1024 devices in a mesh: mapx: 16 (over z_lo, core), mapy: 16 (over z_hi, x), layer: 4 (over y).
Axes of the slice: x: 4, y: 4, z: 32 (z_hi: 4, z_lo: 8; z = z_hi * 8 + z_lo), core: 2. Of those that a mesh axis runs over, the one named last changes fastest.
Arguments:
- velocity: float32 [16, 2, 8, 128, 2048], P(None, None, 'layer', 'mapx', 'mapy'), may hold values from -6 to 6
- viscosity: float32 [8, 128, 2048], P('layer', 'mapx', 'mapy'), may hold values from 0.5 to 5
- friction: float32 [128, 2048], P('mapx', 'mapy'), may hold values from 0.05 to 0.5
- owner: int32 [16, 16, 1024, 1], P('mapx', 'mapy'), may hold values from 0 to 63; in each aligned block of 1024 rows (0 to 1023, 1024 to 2047, ..., all dimensions but the last counted through in order) at most 32 rows name the same one
- cell: int32 [16, 16, 1024], P('mapx', 'mapy'), may hold values from 0 to 511
- directions: float32 [16, 64, 8192], P(None, 'mapx', ('mapy', 'layer')), may hold values from -6 to 6
- stiffness: float32 [64, 8192], P('mapx', ('mapy', 'layer')), may hold values from 0.02 to 0.2
Outputs:
- image: float32 [16, 2, 8, 128, 2048], P(None, None, 'layer', 'mapx', 'mapy')
- hessian: float32 [16, 64, 8192], P(None, 'mapx', ('mapy', 'layer'))
The draws below stay inside these ranges and needn't reach their ends.
Inputs may be any that keep to these rules, and one draw needn't show every extreme that they name: Among the faces of one mesh block (aligned blocks of 1024 rows) no owner is named more than 32 times, a bound that some block reaches.
All inputs are finite; a program needn't handle non-finite values.
Results may differ from the reference program's by a relative error of at most 0.00002.
Values sent between devices are 32-bit elements; how exact they have to be, the bound alone decides.
No kernel may reach another device: no remote copies, remote signals or barrier semaphores. Data moves between devices by JAX's collectives and lax.ppermute only.
A program may use at most 32 MiB of HBM per device.

```python
import math
import jax
import jax.numpy as jnp
import numpy as np
from jax import lax

PROBES = 16
CX = 8
CY = 128
MXD = 4
MYD = 128
NX = 128
NY = 2048
NZ = 8
FACES = 1024
OWNERS = 64
CAP = 32
M_DEV = 512
MX = 64
MY = 8192
N_MAPX = 16
N_MAPY = 16


def place_ends(entries, key, least, high):
    extent = entries.shape
    index_at = [jax.random.randint(jax.random.fold_in(key, axis), (), 0, extent[axis]) for axis in range(len(extent))]
    entries = entries.at[tuple(index_at)].set(least)
    longest = extent.index(max(extent))
    index_at[longest] = (index_at[longest] + 1) % extent[longest]
    return entries.at[tuple(index_at)].set(high)


def shard_levels(own_key, dims, split, low, top_value):
    level = 1.0
    for axis_at, blocks in split:
        draws = jax.random.uniform(jax.random.fold_in(jax.random.fold_in(own_key, 6), axis_at), (blocks,), jnp.float32, low / len(split), top_value / len(split))
        level = level * jnp.repeat(jnp.exp(draws), dims[axis_at] // blocks).reshape((-1,) + (1,) * (len(dims) - 1 - axis_at))
    return level


def shared_out(rng, own, number, rows, amount, top, limit, skew):
    ranking = jax.random.permutation(rng, amount)
    crowded, ordinary = portions_of(amount, rows * top, limit, skew, True), portions_of(amount, rows * top, limit, skew, False)
    places = jnp.arange(amount)

    def named(lengths, rotation):
        used = int((lengths > 0).sum())
        fixed = max(1, used // 4)
        passed = fixed + (places - fixed + rotation * (used - fixed)) % max(1, amount - fixed)
        return jnp.zeros((amount,), jnp.int32).at[ranking[jnp.where(places < fixed, places, passed)]].set(jnp.asarray(lengths, jnp.int32))

    lengths = jnp.where(number % 4 == 0, named(crowded, number // 4), named(ordinary, number - number // 4 - 1))
    mixed = jax.random.permutation(jax.random.fold_in(own, 3), amount)
    source_of, receiver = mixed[0:amount // 2 * 2:2], mixed[1:amount // 2 * 2:2]
    room = jnp.minimum(lengths[source_of] - 1, limit - lengths[receiver]) // 2
    room = jnp.where((source_of == ranking[0]) | (receiver == ranking[0]) | (lengths[receiver] == 0), 0, jnp.maximum(room, 0))
    passed = jax.random.randint(jax.random.fold_in(own, 4), (amount // 2,), 0, 1 << 20) % (room + 1)
    lengths = lengths.at[source_of].add(-passed).at[receiver].add(passed)
    items = jnp.searchsorted(jnp.cumsum(lengths), jnp.arange(rows * top), side="right").astype(jnp.int32)
    grid = items.reshape(top, rows).T
    grid = grid[jax.random.permutation(jax.random.fold_in(own, 1), rows)]
    rotation = jax.random.randint(jax.random.fold_in(own, 2), (rows, 1), 0, top)
    return jnp.take_along_axis(grid, (jnp.arange(top)[None, :] + rotation) % top, axis=1)


def portions_of(amount, total, bound, slope, full):
    weights = [(1 << 20) // math.isqrt(rank ** slope) + 1 for rank in range(1, amount + 1)]
    largest = bound if full else min(bound, max(-(-total // amount), total * weights[0] // sum(weights)))
    least = 1 if total - largest >= amount - 1 else 0
    holding, spare = [largest] + [least] * (amount - 1), total - largest - least * (amount - 1)
    while spare > 0:
        candidates = [i for i in range(1, amount) if holding[i] < largest] or [i for i in range(1, amount) if holding[i] < bound]
        pool, budget = sum([weights[i] for i in candidates]), spare
        for i in candidates:
            addition = min(bound - holding[i], max(1, budget * weights[i] // pool), spare)
            holding[i] = holding[i] + addition
            spare = spare - addition
    return np.array(holding)


def scatter_about(own_key, shape, deviation, reach, shards=(), kind=jnp.bfloat16):
    level = shard_levels(own_key, shape, shards, -0.22, 0.18) if shards else 1.0
    result = jax.random.normal(own_key, shape, jnp.float32) * deviation * level
    return jnp.minimum(jnp.maximum(result, -reach), reach).astype(kind)


def setup_inputs(seed: int = 0) -> dict:
    splits = jax.random.split(jax.random.key(seed), 8)
    velocity = scatter_about(splits[0], (PROBES, 2, NZ, NX, NY), 1.0, 6.0, ((2, 4), (3, 16), (4, 16)), jnp.float32)
    viscosity = jnp.clip(jnp.exp(math.log(5.0) - 2.3025851 * jax.random.uniform(splits[1], (NZ, NX, NY), jnp.float32) ** shard_levels(splits[1], (NZ, NX, NY), ((0, 4), (1, 16), (2, 16)), -0.2, 0.2)), 0.5, 5.0)
    friction = jnp.clip(jnp.exp(math.log(0.5) - 2.3025851 * jax.random.uniform(splits[2], (NX, NY), jnp.float32) ** shard_levels(splits[2], (NX, NY), ((0, 16), (1, 16)), -0.2, 0.2)), 0.05, 0.5)
    owner_keys = jax.random.split(jax.random.fold_in(splits[3], 1), N_MAPX * N_MAPY * FACES // FACES)
    owner_turns = jax.random.permutation(jax.random.fold_in(splits[3], 3), N_MAPX * N_MAPY * FACES // FACES)
    owner = jax.vmap(lambda own, number: shared_out(jax.random.fold_in(splits[3], 2), own, number, FACES, OWNERS, 1, CAP, 2))(owner_keys, owner_turns).reshape((N_MAPX, N_MAPY, FACES, 1))
    cell = place_ends(jax.random.randint(splits[4], (N_MAPX, N_MAPY, FACES), 0, M_DEV), jax.random.fold_in(splits[4], 1), 0, M_DEV - 1).astype(jnp.int32)
    directions = scatter_about(splits[5], (PROBES, MX, MY), 1.0, 6.0, ((1, 16), (2, 64)), jnp.float32)
    stiffness = jnp.clip(jnp.exp(math.log(0.2) - 2.3025851 * jax.random.uniform(splits[6], (MX, MY), jnp.float32) ** shard_levels(splits[6], (MX, MY), ((0, 16), (1, 64)), -0.2, 0.2)), 0.02, 0.2)
    return dict(velocity=velocity, viscosity=viscosity, friction=friction, owner=owner, cell=cell, directions=directions, stiffness=stiffness)


def stencil(padded, viscous):
    center = padded[..., 1:-1, 1:-1, 1:-1]
    visc = viscous[1:-1, 1:-1, 1:-1]
    weight_x = jnp.array([1.0, 0.25], jnp.float32)[:, None, None, None]
    weight_y = jnp.array([0.25, 1.0], jnp.float32)[:, None, None, None]
    total = 2.0 * 0.5 * (visc + viscous[2:, 1:-1, 1:-1]) * (center - padded[..., 2:, 1:-1, 1:-1])
    total = total + 2.0 * 0.5 * (visc + viscous[:-2, 1:-1, 1:-1]) * (center - padded[..., :-2, 1:-1, 1:-1])
    total = total + weight_x * 0.5 * (visc + viscous[1:-1, 2:, 1:-1]) * (center - padded[..., 1:-1, 2:, 1:-1])
    total = total + weight_x * 0.5 * (visc + viscous[1:-1, :-2, 1:-1]) * (center - padded[..., 1:-1, :-2, 1:-1])
    total = total + weight_y * 0.5 * (visc + viscous[1:-1, 1:-1, 2:]) * (center - padded[..., 1:-1, 1:-1, 2:])
    total = total + weight_y * 0.5 * (visc + viscous[1:-1, 1:-1, :-2]) * (center - padded[..., 1:-1, 1:-1, :-2])
    return total


def laplace(padded):
    return 4.0 * padded[..., 1:-1, 1:-1] - padded[..., 2:, 1:-1] - padded[..., :-2, 1:-1] - padded[..., 1:-1, 2:] - padded[..., 1:-1, :-2]


def pad_map(field):
    return jnp.pad(field, ((0, 0), (1, 1), (1, 1)))


def reference(velocity, viscosity, friction, owner, cell, directions, stiffness):
    viscous = jnp.pad(viscosity, 1)

    def one_probe(field):
        return stencil(jnp.pad(field, ((0, 0), (1, 1), (1, 1), (1, 1))), viscous)

    image = lax.map(one_probe, velocity)
    trace = friction * (image[:, 0, 0] + image[:, 1, 0])
    probes = trace.shape[0]
    blocked = trace.reshape(probes, N_MAPX, CX, N_MAPY, CY).transpose(0, 1, 3, 2, 4)
    blocked = blocked.reshape(probes, N_MAPX, N_MAPY * FACES)
    target = owner[..., 0].reshape(N_MAPX, N_MAPY * FACES)
    local = cell.reshape(N_MAPX, N_MAPY * FACES)
    map_row = local // MYD
    map_col = target * MYD + local % MYD
    block_index = jnp.broadcast_to(jnp.arange(N_MAPX, dtype=jnp.int32)[:, None], map_row.shape)
    data = jnp.zeros((probes, N_MAPX, MXD, MY), jnp.float32)
    data = data.at[:, block_index, map_row, map_col].add(blocked)
    data = data.reshape(probes, MX, MY)
    inner = stiffness[None] * laplace(pad_map(directions))
    prior = laplace(pad_map(inner)) + 0.1 * directions
    return image, data + prior
```

```python
import jax
import jax.numpy as jnp
from jax import lax
from jax.sharding import PartitionSpec as P


def halo_pair(cells, axis, dim):
    count = lax.axis_size(axis)
    head = lax.slice_in_dim(cells, 0, 1, axis=dim)
    tail = lax.slice_in_dim(cells, cells.shape[dim] - 1, cells.shape[dim], axis=dim)
    low = lax.ppermute(tail, axis, [(i, i + 1) for i in range(count - 1)])
    high = lax.ppermute(head, axis, [(i + 1, i) for i in range(count - 1)])
    return low, high


def pad_others(part, lead, done):
    widths = [(0, 0)] * part.ndim
    for dim in done:
        widths[dim] = (1, 1)
    return jnp.pad(part, widths) if done else part


def with_faces(cells, sides):
    parts = [halo_pair(cells, axis, dim) for axis, dim in sides]
    done = []
    for (axis, dim), (low, high) in zip(sides, parts):
        cells = jnp.concatenate(
            [pad_others(low, 0, done), cells, pad_others(high, 0, done)], axis=dim
        )
        done.append(dim)
    return cells


def stencil(padded, viscous):
    center = padded[..., 1:-1, 1:-1, 1:-1]
    visc = viscous[1:-1, 1:-1, 1:-1]
    weight_x = jnp.array([1.0, 0.25], jnp.float32)[:, None, None, None]
    weight_y = jnp.array([0.25, 1.0], jnp.float32)[:, None, None, None]
    total = 2.0 * 0.5 * (visc + viscous[2:, 1:-1, 1:-1]) * (center - padded[..., 2:, 1:-1, 1:-1])
    total = total + 2.0 * 0.5 * (visc + viscous[:-2, 1:-1, 1:-1]) * (
        center - padded[..., :-2, 1:-1, 1:-1]
    )
    total = total + weight_x * 0.5 * (visc + viscous[1:-1, 2:, 1:-1]) * (
        center - padded[..., 1:-1, 2:, 1:-1]
    )
    total = total + weight_x * 0.5 * (visc + viscous[1:-1, :-2, 1:-1]) * (
        center - padded[..., 1:-1, :-2, 1:-1]
    )
    total = total + weight_y * 0.5 * (visc + viscous[1:-1, 1:-1, 2:]) * (
        center - padded[..., 1:-1, 1:-1, 2:]
    )
    total = total + weight_y * 0.5 * (visc + viscous[1:-1, 1:-1, :-2]) * (
        center - padded[..., 1:-1, 1:-1, :-2]
    )
    return total


def laplace(padded):
    return (
        4.0 * padded[..., 1:-1, 1:-1]
        - padded[..., 2:, 1:-1]
        - padded[..., :-2, 1:-1]
        - padded[..., 1:-1, 2:]
        - padded[..., 1:-1, :-2]
    )


def map_border(field):
    return with_faces(field, (("mapx", 1), (("mapy", "layer"), 2)))


def from_bottom(x, axis):
    count = lax.axis_size(axis)
    mine = lax.axis_index(axis) == 0
    total = jnp.where(mine, x, jnp.zeros_like(x))
    for to in range(1, count):
        total = total + lax.ppermute(x, axis, [(0, to)])
    return total


def slot_places(keys, group_count, capacity, keep):
    onehot = (
        (keys[:, None] == jnp.arange(group_count, dtype=jnp.int32)[None, :]) & keep[:, None]
    ).astype(jnp.int32)
    before = jnp.cumsum(onehot, axis=0) - onehot
    slot_index = jnp.sum(before * onehot, axis=1)
    return jnp.where(keep, keys * capacity + slot_index, group_count * capacity)


def shards(velocity, viscosity, friction, owner, cell, directions, stiffness):
    probes = velocity.shape[0]
    depth, rows, cols = viscosity.shape
    stacked = jnp.concatenate([velocity.reshape(probes * 2, depth, rows, cols), viscosity[None]], 0)
    extended = with_faces(stacked, (("layer", 1), ("mapx", 2), ("mapy", 3)))
    padded = extended[:-1].reshape(probes, 2, depth + 2, rows + 2, cols + 2)
    image = stencil(padded, extended[-1])
    face_count = rows * cols
    face_rows = (friction * (image[:, 0, 0] + image[:, 1, 0])).reshape(probes, face_count).T
    targets = owner.reshape(face_count)
    local_cells = cell.reshape(face_count).astype(jnp.float32)
    count_y = lax.axis_size("mapy")
    count_layer = lax.axis_size("layer")
    owner_count = count_y * count_layer
    capacity = 2 * face_count // owner_count
    my_layer = lax.axis_index("layer")
    spread = from_bottom(face_rows, "layer")
    keep = targets % count_layer == my_layer
    position = slot_places(targets // count_layer, count_y, capacity, keep)
    total_slots = count_y * capacity
    rows_out = jnp.concatenate([spread, local_cells[:, None]], axis=1)
    packed = (
        jnp.zeros((total_slots + 1, probes + 1), jnp.float32).at[position].set(rows_out)[:total_slots]
    )
    got = lax.all_to_all(
        packed.reshape(count_y, capacity, probes + 1),
        "mapy",
        split_axis=0,
        concat_axis=0,
        tiled=True,
    ).reshape(-1, probes + 1)
    map_rows = directions.shape[1]
    map_cols = directions.shape[2]
    summed = jax.ops.segment_sum(
        got[:, :probes],
        got[:, probes].astype(jnp.int32),
        num_segments=map_rows * map_cols,
    )
    data = summed.T.reshape(probes, map_rows, map_cols)
    inner = stiffness[None] * laplace(map_border(directions))
    prior = laplace(map_border(inner))
    hessian = data + prior + 0.1 * directions
    return (image, hessian)


def solution(mesh):
    return jax.shard_map(
        shards,
        mesh=mesh,
        in_specs=(
            P(None, None, "layer", "mapx", "mapy"),
            P("layer", "mapx", "mapy"),
            P("mapx", "mapy"),
            P("mapx", "mapy", None, None),
            P("mapx", "mapy", None),
            P(None, "mapx", ("mapy", "layer")),
            P("mapx", ("mapy", "layer")),
        ),
        out_specs=(P(None, None, "layer", "mapx", "mapy"), P(None, "mapx", ("mapy", "layer"))),
        check_vma=False,
    )
```

```python
import jax
import jax.numpy as jnp
from jax import lax
from jax.sharding import PartitionSpec as P


def send(parts, axis, pairs):
    flat = jnp.concatenate([p.reshape(-1) for p in parts])
    got = lax.ppermute(flat, axis, pairs)
    out, at = [], 0
    for p in parts:
        out.append(got[at : at + p.size].reshape(p.shape))
        at += p.size
    return out


def steps(count):
    return [(i, i + 1) for i in range(count - 1)], [(i + 1, i) for i in range(count - 1)]


def pad_dims(part, dims):
    widths = [(0, 0)] * part.ndim
    for dim in dims:
        widths[dim] = (1, 1)
    return jnp.pad(part, widths)


def stencil(padded, viscous):
    center = padded[..., 1:-1, 1:-1, 1:-1]
    visc = viscous[1:-1, 1:-1, 1:-1]
    weight_x = jnp.array([1.0, 0.25], jnp.float32)[:, None, None, None]
    weight_y = jnp.array([0.25, 1.0], jnp.float32)[:, None, None, None]
    total = 2.0 * 0.5 * (visc + viscous[2:, 1:-1, 1:-1]) * (center - padded[..., 2:, 1:-1, 1:-1])
    total = total + 2.0 * 0.5 * (visc + viscous[:-2, 1:-1, 1:-1]) * (
        center - padded[..., :-2, 1:-1, 1:-1]
    )
    total = total + weight_x * 0.5 * (visc + viscous[1:-1, 2:, 1:-1]) * (
        center - padded[..., 1:-1, 2:, 1:-1]
    )
    total = total + weight_x * 0.5 * (visc + viscous[1:-1, :-2, 1:-1]) * (
        center - padded[..., 1:-1, :-2, 1:-1]
    )
    total = total + weight_y * 0.5 * (visc + viscous[1:-1, 1:-1, 2:]) * (
        center - padded[..., 1:-1, 1:-1, 2:]
    )
    total = total + weight_y * 0.5 * (visc + viscous[1:-1, 1:-1, :-2]) * (
        center - padded[..., 1:-1, 1:-1, :-2]
    )
    return total


def laplace(padded):
    return (
        4.0 * padded[..., 1:-1, 1:-1]
        - padded[..., 2:, 1:-1]
        - padded[..., :-2, 1:-1]
        - padded[..., 1:-1, 2:]
        - padded[..., 1:-1, :-2]
    )


def from_bottom(x, axis):
    count = lax.axis_size(axis)
    mine = lax.axis_index(axis) == 0
    total = jnp.where(mine, x, jnp.zeros_like(x))
    for to in range(1, count):
        total = total + lax.ppermute(x, axis, [(0, to)])
    return total


def slot_places(keys, group_count, capacity, keep):
    onehot = (
        (keys[:, None] == jnp.arange(group_count, dtype=jnp.int32)[None, :]) & keep[:, None]
    ).astype(jnp.int32)
    before = jnp.cumsum(onehot, axis=0) - onehot
    slot_index = jnp.sum(before * onehot, axis=1)
    return jnp.where(keep, keys * capacity + slot_index, group_count * capacity)


def corner_pairs(rows, cols, step_row, step_col):
    pairs = []
    for a in range(rows):
        for j in range(cols):
            if 0 <= a - step_row < rows and 0 <= j - step_col < cols:
                pairs.append(((a - step_row) * cols + (j - step_col), a * cols + j))
    return pairs


def shards(velocity, viscosity, friction, owner, cell, directions, stiffness):
    probes = velocity.shape[0]
    depth, rows, cols = viscosity.shape
    column = ("mapy", "layer")
    every = ("mapx", "mapy", "layer")
    count_x = lax.axis_size("mapx")
    count_col = lax.axis_size(column)
    count_layer = lax.axis_size("layer")
    my_layer = lax.axis_index("layer")
    stacked = jnp.concatenate([velocity.reshape(probes * 2, depth, rows, cols), viscosity[None]], 0)
    fwd_x, bwd_x = steps(count_x)
    fwd_c, bwd_c = steps(count_col)
    fwd_y, bwd_y = steps(lax.axis_size("mapy"))
    d, k = directions, stiffness
    x_lo = send([stacked[:, :, -1:], d[:, -2:], k[-1:]], "mapx", fwd_x)
    x_hi = send([stacked[:, :, :1], d[:, :2], k[:1]], "mapx", bwd_x)
    c_lo = send([stacked[:, -1:], d[:, :, -2:], k[:, -1:]], column, fwd_c)
    c_hi = send([stacked[:, :1], d[:, :, :2], k[:, :1]], column, bwd_c)
    (y_lo,) = send([stacked[..., -1:]], "mapy", fwd_y)
    (y_hi,) = send([stacked[..., :1]], "mapy", bwd_y)
    corner = {}
    for sr, sc, src in ((1, 1, d[:, -1, -1]), (1, -1, d[:, -1, 0]), (-1, 1, d[:, 0, -1]), (-1, -1, d[:, 0, 0])):
        corner[sr, sc] = lax.ppermute(src, every, corner_pairs(count_x, count_col, sr, sc))[:, None, None]

    z_lo = jnp.where(my_layer > 0, c_lo[0], jnp.zeros_like(c_lo[0]))
    z_hi = jnp.where(my_layer < count_layer - 1, c_hi[0], jnp.zeros_like(c_hi[0]))
    extended = jnp.concatenate([z_lo, stacked, z_hi], axis=1)
    extended = jnp.concatenate([pad_dims(x_lo[0], (1,)), extended, pad_dims(x_hi[0], (1,))], axis=2)
    extended = jnp.concatenate([pad_dims(y_lo, (1, 2)), extended, pad_dims(y_hi, (1, 2))], axis=3)
    padded = extended[:-1].reshape(probes, 2, depth + 2, rows + 2, cols + 2)
    image = stencil(padded, extended[-1])

    zero2 = jnp.zeros((probes, 1, 2), jnp.float32)
    zero1 = jnp.zeros((probes, 1, 1), jnp.float32)
    top = jnp.concatenate(
        [
            jnp.concatenate([zero2, x_lo[1][:, :1], zero2], axis=2),
            jnp.concatenate([zero1, corner[1, 1], x_lo[1][:, 1:], corner[1, -1], zero1], axis=2),
        ],
        axis=1,
    )
    bottom = jnp.concatenate(
        [
            jnp.concatenate([zero1, corner[-1, 1], x_hi[1][:, :1], corner[-1, -1], zero1], axis=2),
            jnp.concatenate([zero2, x_hi[1][:, 1:], zero2], axis=2),
        ],
        axis=1,
    )
    middle = jnp.concatenate([c_lo[1], d, c_hi[1]], axis=2)
    wide = jnp.concatenate([top, middle, bottom], axis=1)
    ring = jnp.concatenate(
        [
            pad_dims(x_lo[2], (1,)),
            jnp.concatenate([c_lo[2], k, c_hi[2]], axis=1),
            pad_dims(x_hi[2], (1,)),
        ],
        axis=0,
    )
    inner = ring[None] * laplace(wide)
    prior = laplace(inner)

    face_count = rows * cols
    face_rows = (friction * (image[:, 0, 0] + image[:, 1, 0])).reshape(probes, face_count).T
    targets = owner.reshape(face_count)
    local_cells = cell.reshape(face_count).astype(jnp.float32)
    count_y = lax.axis_size("mapy")
    owner_count = count_y * count_layer
    capacity = 2 * face_count // owner_count
    spread = from_bottom(face_rows, "layer")
    keep = targets % count_layer == my_layer
    position = slot_places(targets // count_layer, count_y, capacity, keep)
    total_slots = count_y * capacity
    rows_out = jnp.concatenate([spread, local_cells[:, None]], axis=1)
    packed = (
        jnp.zeros((total_slots + 1, probes + 1), jnp.float32).at[position].set(rows_out)[:total_slots]
    )
    got = lax.all_to_all(
        packed.reshape(count_y, capacity, probes + 1),
        "mapy",
        split_axis=0,
        concat_axis=0,
        tiled=True,
    ).reshape(-1, probes + 1)
    map_rows = directions.shape[1]
    map_cols = directions.shape[2]
    summed = jax.ops.segment_sum(
        got[:, :probes],
        got[:, probes].astype(jnp.int32),
        num_segments=map_rows * map_cols,
    )
    data = summed.T.reshape(probes, map_rows, map_cols)
    hessian = data + prior + 0.1 * directions
    return (image, hessian)


def solution(mesh):
    return jax.shard_map(
        shards,
        mesh=mesh,
        in_specs=(
            P(None, None, "layer", "mapx", "mapy"),
            P("layer", "mapx", "mapy"),
            P("mapx", "mapy"),
            P("mapx", "mapy", None, None),
            P("mapx", "mapy", None),
            P(None, "mapx", ("mapy", "layer")),
            P("mapx", ("mapy", "layer")),
        ),
        out_specs=(P(None, None, "layer", "mapx", "mapy"), P(None, "mapx", ("mapy", "layer"))),
        check_vma=False,
    )
```

```python
import jax
import jax.numpy as jnp
from jax import lax
from jax.sharding import PartitionSpec as P


def halo_pair(cells, axis, dim):
    count = lax.axis_size(axis)
    head = lax.slice_in_dim(cells, 0, 1, axis=dim)
    tail = lax.slice_in_dim(cells, cells.shape[dim] - 1, cells.shape[dim], axis=dim)
    low = lax.ppermute(tail, axis, [(i, i + 1) for i in range(count - 1)])
    high = lax.ppermute(head, axis, [(i + 1, i) for i in range(count - 1)])
    return low, high


def pad_others(part, lead, done):
    widths = [(0, 0)] * part.ndim
    for dim in done:
        widths[dim] = (1, 1)
    return jnp.pad(part, widths) if done else part


def with_faces(cells, sides):
    parts = [halo_pair(cells, axis, dim) for axis, dim in sides]
    done = []
    for (axis, dim), (low, high) in zip(sides, parts):
        cells = jnp.concatenate(
            [pad_others(low, 0, done), cells, pad_others(high, 0, done)], axis=dim
        )
        done.append(dim)
    return cells


def stencil(padded, viscous):
    center = padded[..., 1:-1, 1:-1, 1:-1]
    visc = viscous[1:-1, 1:-1, 1:-1]
    weight_x = jnp.array([1.0, 0.25], jnp.float32)[:, None, None, None]
    weight_y = jnp.array([0.25, 1.0], jnp.float32)[:, None, None, None]
    total = 2.0 * 0.5 * (visc + viscous[2:, 1:-1, 1:-1]) * (center - padded[..., 2:, 1:-1, 1:-1])
    total = total + 2.0 * 0.5 * (visc + viscous[:-2, 1:-1, 1:-1]) * (
        center - padded[..., :-2, 1:-1, 1:-1]
    )
    total = total + weight_x * 0.5 * (visc + viscous[1:-1, 2:, 1:-1]) * (
        center - padded[..., 1:-1, 2:, 1:-1]
    )
    total = total + weight_x * 0.5 * (visc + viscous[1:-1, :-2, 1:-1]) * (
        center - padded[..., 1:-1, :-2, 1:-1]
    )
    total = total + weight_y * 0.5 * (visc + viscous[1:-1, 1:-1, 2:]) * (
        center - padded[..., 1:-1, 1:-1, 2:]
    )
    total = total + weight_y * 0.5 * (visc + viscous[1:-1, 1:-1, :-2]) * (
        center - padded[..., 1:-1, 1:-1, :-2]
    )
    return total


def laplace(padded):
    return (
        4.0 * padded[..., 1:-1, 1:-1]
        - padded[..., 2:, 1:-1]
        - padded[..., :-2, 1:-1]
        - padded[..., 1:-1, 2:]
        - padded[..., 1:-1, :-2]
    )


def map_border(field):
    return with_faces(field, (("mapx", 1), (("mapy", "layer"), 2)))


def from_bottom(x, axis):
    count = lax.axis_size(axis)
    mine = lax.axis_index(axis) == 0
    total = jnp.where(mine, x, jnp.zeros_like(x))
    for to in range(1, count):
        total = total + lax.ppermute(x, axis, [(0, to)])
    return total


def slot_places(keys, group_count, capacity, keep):
    onehot = (
        (keys[:, None] == jnp.arange(group_count, dtype=jnp.int32)[None, :]) & keep[:, None]
    ).astype(jnp.int32)
    before = jnp.cumsum(onehot, axis=0) - onehot
    slot_index = jnp.sum(before * onehot, axis=1)
    return jnp.where(keep, keys * capacity + slot_index, group_count * capacity)


def shards(velocity, viscosity, friction, owner, cell, directions, stiffness):
    probes = velocity.shape[0]
    depth, rows, cols = viscosity.shape
    stacked = jnp.concatenate([velocity.reshape(probes * 2, depth, rows, cols), viscosity[None]], 0)
    extended = with_faces(stacked, (("layer", 1), ("mapx", 2), ("mapy", 3)))
    padded = extended[:-1].reshape(probes, 2, depth + 2, rows + 2, cols + 2)
    image = stencil(padded, extended[-1])
    face_count = rows * cols
    face_rows = (friction * (image[:, 0, 0] + image[:, 1, 0])).reshape(probes, face_count).T
    targets = owner.reshape(face_count)
    local_cells = cell.reshape(face_count).astype(jnp.float32)
    count_y = lax.axis_size("mapy")
    count_layer = lax.axis_size("layer")
    owner_count = count_y * count_layer
    capacity = 2 * face_count // owner_count
    my_layer = lax.axis_index("layer")
    spread = from_bottom(face_rows, "layer")
    keep = targets % count_layer == my_layer
    position = slot_places(targets // count_layer, count_y, capacity, keep)
    total_slots = count_y * capacity
    rows_out = jnp.concatenate([spread, local_cells[:, None]], axis=1)
    packed = (
        jnp.zeros((total_slots + 1, probes + 1), jnp.float32).at[position].set(rows_out)[:total_slots]
    )
    got = lax.all_to_all(
        packed.reshape(count_y, capacity, probes + 1),
        "mapy",
        split_axis=0,
        concat_axis=0,
        tiled=True,
    ).reshape(-1, probes + 1)
    map_rows = directions.shape[1]
    map_cols = directions.shape[2]
    summed = jax.ops.segment_sum(
        got[:, :probes],
        got[:, probes].astype(jnp.int32),
        num_segments=map_rows * map_cols,
    )
    data = summed.T.reshape(probes, map_rows, map_cols)
    directions, stiffness, got = lax.optimization_barrier((directions, stiffness, got))
    inner = stiffness[None] * laplace(map_border(directions))
    prior = laplace(map_border(inner))
    hessian = data + prior + 0.1 * directions
    return (image, hessian)


def solution(mesh):
    return jax.shard_map(
        shards,
        mesh=mesh,
        in_specs=(
            P(None, None, "layer", "mapx", "mapy"),
            P("layer", "mapx", "mapy"),
            P("mapx", "mapy"),
            P("mapx", "mapy", None, None),
            P("mapx", "mapy", None),
            P(None, "mapx", ("mapy", "layer")),
            P("mapx", ("mapy", "layer")),
        ),
        out_specs=(P(None, None, "layer", "mapx", "mapy"), P(None, "mapx", ("mapy", "layer"))),
        check_vma=False,
    )
```

```python
import jax
import jax.numpy as jnp
from jax import lax
from jax.sharding import PartitionSpec as P


def send(parts, axis, pairs):
    flat = jnp.concatenate([p.reshape(-1) for p in parts])
    got = lax.ppermute(flat, axis, pairs)
    out, at = [], 0
    for p in parts:
        out.append(got[at : at + p.size].reshape(p.shape))
        at += p.size
    return out


def steps(count):
    return [(i, i + 1) for i in range(count - 1)], [(i + 1, i) for i in range(count - 1)]


def pad_dims(part, dims):
    widths = [(0, 0)] * part.ndim
    for dim in dims:
        widths[dim] = (1, 1)
    return jnp.pad(part, widths)


def stencil(padded, viscous):
    center = padded[..., 1:-1, 1:-1, 1:-1]
    visc = viscous[1:-1, 1:-1, 1:-1]
    weight_x = jnp.array([1.0, 0.25], jnp.float32)[:, None, None, None]
    weight_y = jnp.array([0.25, 1.0], jnp.float32)[:, None, None, None]
    total = 2.0 * 0.5 * (visc + viscous[2:, 1:-1, 1:-1]) * (center - padded[..., 2:, 1:-1, 1:-1])
    total = total + 2.0 * 0.5 * (visc + viscous[:-2, 1:-1, 1:-1]) * (
        center - padded[..., :-2, 1:-1, 1:-1]
    )
    total = total + weight_x * 0.5 * (visc + viscous[1:-1, 2:, 1:-1]) * (
        center - padded[..., 1:-1, 2:, 1:-1]
    )
    total = total + weight_x * 0.5 * (visc + viscous[1:-1, :-2, 1:-1]) * (
        center - padded[..., 1:-1, :-2, 1:-1]
    )
    total = total + weight_y * 0.5 * (visc + viscous[1:-1, 1:-1, 2:]) * (
        center - padded[..., 1:-1, 1:-1, 2:]
    )
    total = total + weight_y * 0.5 * (visc + viscous[1:-1, 1:-1, :-2]) * (
        center - padded[..., 1:-1, 1:-1, :-2]
    )
    return total


def laplace(padded):
    return (
        4.0 * padded[..., 1:-1, 1:-1]
        - padded[..., 2:, 1:-1]
        - padded[..., :-2, 1:-1]
        - padded[..., 1:-1, 2:]
        - padded[..., 1:-1, :-2]
    )


def from_bottom(x, axis):
    count = lax.axis_size(axis)
    mine = lax.axis_index(axis) == 0
    total = jnp.where(mine, x, jnp.zeros_like(x))
    for to in range(1, count):
        total = total + lax.ppermute(x, axis, [(0, to)])
    return total


def slot_places(keys, group_count, capacity, keep):
    onehot = (
        (keys[:, None] == jnp.arange(group_count, dtype=jnp.int32)[None, :]) & keep[:, None]
    ).astype(jnp.int32)
    before = jnp.cumsum(onehot, axis=0) - onehot
    slot_index = jnp.sum(before * onehot, axis=1)
    return jnp.where(keep, keys * capacity + slot_index, group_count * capacity)


def shards(velocity, viscosity, friction, owner, cell, directions, stiffness):
    probes = velocity.shape[0]
    depth, rows, cols = viscosity.shape
    column = ("mapy", "layer")
    count_x = lax.axis_size("mapx")
    count_col = lax.axis_size(column)
    count_layer = lax.axis_size("layer")
    my_layer = lax.axis_index("layer")
    stacked = jnp.concatenate([velocity.reshape(probes * 2, depth, rows, cols), viscosity[None]], 0)
    fwd_x, bwd_x = steps(count_x)
    fwd_c, bwd_c = steps(count_col)
    fwd_y, bwd_y = steps(lax.axis_size("mapy"))
    d = directions
    fwd_l, bwd_l = steps(count_layer)
    x_lo = send([stacked[:, :, -1:], d[:, -1:]], "mapx", fwd_x)
    x_hi = send([stacked[:, :, :1], d[:, :1]], "mapx", bwd_x)
    (z_lo,) = send([stacked[:, -1:]], "layer", fwd_l)
    (z_hi,) = send([stacked[:, :1]], "layer", bwd_l)
    (y_lo,) = send([stacked[..., -1:]], "mapy", fwd_y)
    (y_hi,) = send([stacked[..., :1]], "mapy", bwd_y)
    (c_lo,) = send([d[:, :, -1:]], column, fwd_c)
    (c_hi,) = send([d[:, :, :1]], column, bwd_c)

    extended = jnp.concatenate([z_lo, stacked, z_hi], axis=1)
    extended = jnp.concatenate([pad_dims(x_lo[0], (1,)), extended, pad_dims(x_hi[0], (1,))], axis=2)
    extended = jnp.concatenate([pad_dims(y_lo, (1, 2)), extended, pad_dims(y_hi, (1, 2))], axis=3)
    padded = extended[:-1].reshape(probes, 2, depth + 2, rows + 2, cols + 2)
    image = stencil(padded, extended[-1])

    wide = jnp.concatenate([x_lo[1], d, x_hi[1]], axis=1)
    wide = jnp.concatenate([pad_dims(c_lo, (1,)), wide, pad_dims(c_hi, (1,))], axis=2)
    inner = stiffness[None] * laplace(wide)
    (i_up,) = send([inner[:, -1:]], "mapx", fwd_x)
    (i_down,) = send([inner[:, :1]], "mapx", bwd_x)
    (i_left,) = send([inner[:, :, -1:]], column, fwd_c)
    (i_right,) = send([inner[:, :, :1]], column, bwd_c)
    ring = jnp.concatenate([i_up, inner, i_down], axis=1)
    ring = jnp.concatenate([pad_dims(i_left, (1,)), ring, pad_dims(i_right, (1,))], axis=2)
    prior = laplace(ring)

    face_count = rows * cols
    face_rows = (friction * (image[:, 0, 0] + image[:, 1, 0])).reshape(probes, face_count).T
    targets = owner.reshape(face_count)
    local_cells = cell.reshape(face_count).astype(jnp.float32)
    count_y = lax.axis_size("mapy")
    owner_count = count_y * count_layer
    capacity = 2 * face_count // owner_count
    spread = from_bottom(face_rows, "layer")
    keep = targets % count_layer == my_layer
    position = slot_places(targets // count_layer, count_y, capacity, keep)
    total_slots = count_y * capacity
    rows_out = jnp.concatenate([spread, local_cells[:, None]], axis=1)
    packed = (
        jnp.zeros((total_slots + 1, probes + 1), jnp.float32).at[position].set(rows_out)[:total_slots]
    )
    got = lax.all_to_all(
        packed.reshape(count_y, capacity, probes + 1),
        "mapy",
        split_axis=0,
        concat_axis=0,
        tiled=True,
    ).reshape(-1, probes + 1)
    map_rows = directions.shape[1]
    map_cols = directions.shape[2]
    summed = jax.ops.segment_sum(
        got[:, :probes],
        got[:, probes].astype(jnp.int32),
        num_segments=map_rows * map_cols,
    )
    data = summed.T.reshape(probes, map_rows, map_cols)
    hessian = data + prior + 0.1 * directions
    return (image, hessian)


def solution(mesh):
    return jax.shard_map(
        shards,
        mesh=mesh,
        in_specs=(
            P(None, None, "layer", "mapx", "mapy"),
            P("layer", "mapx", "mapy"),
            P("mapx", "mapy"),
            P("mapx", "mapy", None, None),
            P("mapx", "mapy", None),
            P(None, "mapx", ("mapy", "layer")),
            P("mapx", ("mapy", "layer")),
        ),
        out_specs=(P(None, None, "layer", "mapx", "mapy"), P(None, "mapx", ("mapy", "layer"))),
        check_vma=False,
    )
```

```python
import jax
import jax.numpy as jnp
from jax import lax
from jax.sharding import PartitionSpec as P


def send(parts, axis, pairs):
    flat = jnp.concatenate([p.reshape(-1) for p in parts])
    got = lax.ppermute(flat, axis, pairs)
    out, at = [], 0
    for p in parts:
        out.append(got[at : at + p.size].reshape(p.shape))
        at += p.size
    return out


def steps(count):
    return [(i, i + 1) for i in range(count - 1)], [(i + 1, i) for i in range(count - 1)]


def pad_dims(part, dims):
    widths = [(0, 0)] * part.ndim
    for dim in dims:
        widths[dim] = (1, 1)
    return jnp.pad(part, widths)


def stencil(padded, viscous):
    center = padded[..., 1:-1, 1:-1, 1:-1]
    visc = viscous[1:-1, 1:-1, 1:-1]
    weight_x = jnp.array([1.0, 0.25], jnp.float32)[:, None, None, None]
    weight_y = jnp.array([0.25, 1.0], jnp.float32)[:, None, None, None]
    total = 2.0 * 0.5 * (visc + viscous[2:, 1:-1, 1:-1]) * (center - padded[..., 2:, 1:-1, 1:-1])
    total = total + 2.0 * 0.5 * (visc + viscous[:-2, 1:-1, 1:-1]) * (
        center - padded[..., :-2, 1:-1, 1:-1]
    )
    total = total + weight_x * 0.5 * (visc + viscous[1:-1, 2:, 1:-1]) * (
        center - padded[..., 1:-1, 2:, 1:-1]
    )
    total = total + weight_x * 0.5 * (visc + viscous[1:-1, :-2, 1:-1]) * (
        center - padded[..., 1:-1, :-2, 1:-1]
    )
    total = total + weight_y * 0.5 * (visc + viscous[1:-1, 1:-1, 2:]) * (
        center - padded[..., 1:-1, 1:-1, 2:]
    )
    total = total + weight_y * 0.5 * (visc + viscous[1:-1, 1:-1, :-2]) * (
        center - padded[..., 1:-1, 1:-1, :-2]
    )
    return total


def laplace(padded):
    return (
        4.0 * padded[..., 1:-1, 1:-1]
        - padded[..., 2:, 1:-1]
        - padded[..., :-2, 1:-1]
        - padded[..., 1:-1, 2:]
        - padded[..., 1:-1, :-2]
    )


def from_bottom(x, axis):
    count = lax.axis_size(axis)
    mine = lax.axis_index(axis) == 0
    total = jnp.where(mine, x, jnp.zeros_like(x))
    for to in range(1, count):
        total = total + lax.ppermute(x, axis, [(0, to)])
    return total


def slot_places(keys, group_count, capacity, keep):
    onehot = (
        (keys[:, None] == jnp.arange(group_count, dtype=jnp.int32)[None, :]) & keep[:, None]
    ).astype(jnp.int32)
    before = jnp.cumsum(onehot, axis=0) - onehot
    slot_index = jnp.sum(before * onehot, axis=1)
    return jnp.where(keep, keys * capacity + slot_index, group_count * capacity)


def shards(velocity, viscosity, friction, owner, cell, directions, stiffness):
    probes = velocity.shape[0]
    depth, rows, cols = viscosity.shape
    column = ("mapy", "layer")
    count_x = lax.axis_size("mapx")
    count_col = lax.axis_size(column)
    count_layer = lax.axis_size("layer")
    my_layer = lax.axis_index("layer")
    stacked = jnp.concatenate([velocity.reshape(probes * 2, depth, rows, cols), viscosity[None]], 0)
    fwd_x, bwd_x = steps(count_x)
    fwd_c, bwd_c = steps(count_col)
    fwd_y, bwd_y = steps(lax.axis_size("mapy"))
    d = directions
    fwd_l, bwd_l = steps(count_layer)
    x_lo = send([stacked[:, :, -1:], d[:, -1:]], "mapx", fwd_x)
    x_hi = send([stacked[:, :, :1], d[:, :1]], "mapx", bwd_x)
    (z_lo,) = send([stacked[:, -1:]], "layer", fwd_l)
    (z_hi,) = send([stacked[:, :1]], "layer", bwd_l)
    (y_lo,) = send([stacked[..., -1:]], "mapy", fwd_y)
    (y_hi,) = send([stacked[..., :1]], "mapy", bwd_y)
    (c_lo,) = send([d[:, :, -1:]], column, fwd_c)
    (c_hi,) = send([d[:, :, :1]], column, bwd_c)

    extended = jnp.concatenate([z_lo, stacked, z_hi], axis=1)
    extended = jnp.concatenate([pad_dims(x_lo[0], (1,)), extended, pad_dims(x_hi[0], (1,))], axis=2)
    extended = jnp.concatenate([pad_dims(y_lo, (1, 2)), extended, pad_dims(y_hi, (1, 2))], axis=3)
    padded = extended[:-1].reshape(probes, 2, depth + 2, rows + 2, cols + 2)
    image = stencil(padded, extended[-1])

    wide = jnp.concatenate([x_lo[1], d, x_hi[1]], axis=1)
    wide = jnp.concatenate([pad_dims(c_lo, (1,)), wide, pad_dims(c_hi, (1,))], axis=2)
    inner = stiffness[None] * laplace(wide)
    (i_up,) = send([inner[:, -1:]], "mapx", fwd_x)
    (i_down,) = send([inner[:, :1]], "mapx", bwd_x)
    (i_left,) = send([inner[:, :, -1:]], column, fwd_c)
    (i_right,) = send([inner[:, :, :1]], column, bwd_c)
    ring = jnp.concatenate([i_up, inner, i_down], axis=1)
    ring = jnp.concatenate([pad_dims(i_left, (1,)), ring, pad_dims(i_right, (1,))], axis=2)
    prior = laplace(ring)

    face_count = rows * cols
    face_rows = (friction * (image[:, 0, 0] + image[:, 1, 0])).reshape(probes, face_count).T
    targets = owner.reshape(face_count)
    local_cells = cell.reshape(face_count).astype(jnp.float32)
    count_y = lax.axis_size("mapy")
    owner_count = count_y * count_layer
    capacity = 2 * face_count // owner_count
    onehot = (targets[:, None] == jnp.arange(owner_count, dtype=jnp.int32)[None, :]).astype(
        jnp.bfloat16
    )
    order = lax.broadcasted_iota(jnp.int32, (face_count, face_count), 0)
    earlier = (order > lax.broadcasted_iota(jnp.int32, (face_count, face_count), 1)).astype(
        jnp.bfloat16
    )
    before = jnp.dot(earlier, onehot, preferred_element_type=jnp.float32)
    rank = jnp.sum(before * onehot.astype(jnp.float32), axis=1).astype(jnp.int32)
    position = targets * capacity + rank
    total_slots = owner_count * capacity
    rows_out = jnp.concatenate([face_rows, local_cells[:, None]], axis=1)
    packed = jnp.zeros((total_slots, probes + 1), jnp.float32).at[position].set(
        rows_out, mode="drop"
    )
    got = lax.all_to_all(
        packed.reshape(owner_count, capacity, probes + 1),
        column,
        split_axis=0,
        concat_axis=0,
        tiled=True,
    ).reshape(count_y, count_layer, capacity, probes + 1)[:, 0]
    got = got.reshape(-1, probes + 1)
    map_rows = directions.shape[1]
    map_cols = directions.shape[2]
    summed = jax.ops.segment_sum(
        got[:, :probes],
        got[:, probes].astype(jnp.int32),
        num_segments=map_rows * map_cols,
    )
    data = summed.T.reshape(probes, map_rows, map_cols)
    hessian = data + prior + 0.1 * directions
    return (image, hessian)


def solution(mesh):
    return jax.shard_map(
        shards,
        mesh=mesh,
        in_specs=(
            P(None, None, "layer", "mapx", "mapy"),
            P("layer", "mapx", "mapy"),
            P("mapx", "mapy"),
            P("mapx", "mapy", None, None),
            P("mapx", "mapy", None),
            P(None, "mapx", ("mapy", "layer")),
            P("mapx", ("mapy", "layer")),
        ),
        out_specs=(P(None, None, "layer", "mapx", "mapy"), P(None, "mapx", ("mapy", "layer"))),
        check_vma=False,
    )
```

```python
import jax
import jax.numpy as jnp
from jax import lax
from jax.sharding import PartitionSpec as P


def send(parts, axis, pairs):
    flat = jnp.concatenate([p.reshape(-1) for p in parts])
    got = lax.ppermute(flat, axis, pairs)
    out, at = [], 0
    for p in parts:
        out.append(got[at : at + p.size].reshape(p.shape))
        at += p.size
    return out


def steps(count):
    return [(i, i + 1) for i in range(count - 1)], [(i + 1, i) for i in range(count - 1)]


def pad_dims(part, dims):
    widths = [(0, 0)] * part.ndim
    for dim in dims:
        widths[dim] = (1, 1)
    return jnp.pad(part, widths)


def stencil(padded, viscous):
    center = padded[..., 1:-1, 1:-1, 1:-1]
    visc = viscous[1:-1, 1:-1, 1:-1]
    weight_x = jnp.array([1.0, 0.25], jnp.float32)[:, None, None, None]
    weight_y = jnp.array([0.25, 1.0], jnp.float32)[:, None, None, None]
    total = 2.0 * 0.5 * (visc + viscous[2:, 1:-1, 1:-1]) * (center - padded[..., 2:, 1:-1, 1:-1])
    total = total + 2.0 * 0.5 * (visc + viscous[:-2, 1:-1, 1:-1]) * (
        center - padded[..., :-2, 1:-1, 1:-1]
    )
    total = total + weight_x * 0.5 * (visc + viscous[1:-1, 2:, 1:-1]) * (
        center - padded[..., 1:-1, 2:, 1:-1]
    )
    total = total + weight_x * 0.5 * (visc + viscous[1:-1, :-2, 1:-1]) * (
        center - padded[..., 1:-1, :-2, 1:-1]
    )
    total = total + weight_y * 0.5 * (visc + viscous[1:-1, 1:-1, 2:]) * (
        center - padded[..., 1:-1, 1:-1, 2:]
    )
    total = total + weight_y * 0.5 * (visc + viscous[1:-1, 1:-1, :-2]) * (
        center - padded[..., 1:-1, 1:-1, :-2]
    )
    return total


def laplace(padded):
    return (
        4.0 * padded[..., 1:-1, 1:-1]
        - padded[..., 2:, 1:-1]
        - padded[..., :-2, 1:-1]
        - padded[..., 1:-1, 2:]
        - padded[..., 1:-1, :-2]
    )


def from_bottom(x, axis):
    count = lax.axis_size(axis)
    mine = lax.axis_index(axis) == 0
    total = jnp.where(mine, x, jnp.zeros_like(x))
    for to in range(1, count):
        total = total + lax.ppermute(x, axis, [(0, to)])
    return total


def slot_places(keys, group_count, capacity, keep):
    onehot = (
        (keys[:, None] == jnp.arange(group_count, dtype=jnp.int32)[None, :]) & keep[:, None]
    ).astype(jnp.int32)
    before = jnp.cumsum(onehot, axis=0) - onehot
    slot_index = jnp.sum(before * onehot, axis=1)
    return jnp.where(keep, keys * capacity + slot_index, group_count * capacity)


def shards(velocity, viscosity, friction, owner, cell, directions, stiffness):
    probes = velocity.shape[0]
    depth, rows, cols = viscosity.shape
    column = ("mapy", "layer")
    count_x = lax.axis_size("mapx")
    count_col = lax.axis_size(column)
    count_layer = lax.axis_size("layer")
    my_layer = lax.axis_index("layer")
    stacked = jnp.concatenate([velocity.reshape(probes * 2, depth, rows, cols), viscosity[None]], 0)
    fwd_x, bwd_x = steps(count_x)
    fwd_c, bwd_c = steps(count_col)
    fwd_y, bwd_y = steps(lax.axis_size("mapy"))
    d, k = directions, stiffness
    fwd_l, bwd_l = steps(count_layer)
    x_lo = send([stacked[:, :, -1:], d[:, -2:], k[-1:]], "mapx", fwd_x)
    x_hi = send([stacked[:, :, :1], d[:, :2], k[:1]], "mapx", bwd_x)
    (z_lo,) = send([stacked[:, -1:]], "layer", fwd_l)
    (z_hi,) = send([stacked[:, :1]], "layer", bwd_l)
    (y_lo,) = send([stacked[..., -1:]], "mapy", fwd_y)
    (y_hi,) = send([stacked[..., :1]], "mapy", bwd_y)

    extended = jnp.concatenate([z_lo, stacked, z_hi], axis=1)
    extended = jnp.concatenate([pad_dims(x_lo[0], (1,)), extended, pad_dims(x_hi[0], (1,))], axis=2)
    extended = jnp.concatenate([pad_dims(y_lo, (1, 2)), extended, pad_dims(y_hi, (1, 2))], axis=3)
    padded = extended[:-1].reshape(probes, 2, depth + 2, rows + 2, cols + 2)
    image = stencil(padded, extended[-1])

    tall = jnp.concatenate([x_lo[1], d, x_hi[1]], axis=1)
    tall_k = jnp.concatenate([x_lo[2], k, x_hi[2]], axis=0)
    strip_parts = [(tall[:, :, -2:], tall_k[:, -1:]), (tall[:, :, :2], tall_k[:, :1])]

    face_count = rows * cols
    face_rows = (friction * (image[:, 0, 0] + image[:, 1, 0])).reshape(probes, face_count).T
    targets = owner.reshape(face_count)
    local_cells = cell.reshape(face_count).astype(jnp.float32)
    count_y = lax.axis_size("mapy")
    owner_count = count_y * count_layer
    capacity = 2 * face_count // owner_count
    onehot = (targets[:, None] == jnp.arange(owner_count, dtype=jnp.int32)[None, :]).astype(
        jnp.bfloat16
    )
    order = lax.broadcasted_iota(jnp.int32, (face_count, face_count), 0)
    earlier = (order > lax.broadcasted_iota(jnp.int32, (face_count, face_count), 1)).astype(
        jnp.bfloat16
    )
    before = jnp.dot(earlier, onehot, preferred_element_type=jnp.float32)
    rank = jnp.sum(before * onehot.astype(jnp.float32), axis=1).astype(jnp.int32)
    position = targets * capacity + rank
    total_slots = owner_count * capacity
    rows_out = jnp.concatenate([face_rows, local_cells[:, None]], axis=1)
    packed = jnp.zeros((total_slots, probes + 1), jnp.float32).at[position].set(
        rows_out, mode="drop"
    )
    me = lax.axis_index(column)
    strips = [jnp.concatenate([a.reshape(-1), b.reshape(-1)]) for a, b in strip_parts]
    strip_size = strips[0].size
    extra_rows = -(-strip_size // (probes + 1))
    strips = [
        jnp.pad(x, (0, extra_rows * (probes + 1) - strip_size)).reshape(extra_rows, probes + 1)
        for x in strips
    ]
    dest = lax.broadcasted_iota(jnp.int32, (owner_count, 1, 1), 0)
    extra = jnp.where(dest == me + 1, strips[0][None], 0.0) + jnp.where(
        dest == me - 1, strips[1][None], 0.0
    )
    packed = jnp.concatenate([packed.reshape(owner_count, capacity, probes + 1), extra], axis=1)
    received = lax.all_to_all(packed, column, split_axis=0, concat_axis=0, tiled=True)
    got = received[:, :capacity].reshape(count_y, count_layer, capacity, probes + 1)[:, 0]
    got = got.reshape(-1, probes + 1)
    side_lo = lax.dynamic_index_in_dim(received, jnp.maximum(me - 1, 0), 0, keepdims=False)
    side_hi = lax.dynamic_index_in_dim(
        received, jnp.minimum(me + 1, owner_count - 1), 0, keepdims=False
    )
    side_lo = jnp.where(me > 0, side_lo[capacity:], 0.0).reshape(-1)[:strip_size]
    side_hi = jnp.where(me < owner_count - 1, side_hi[capacity:], 0.0).reshape(-1)[:strip_size]
    wide_shape, k_shape = strip_parts[0][0].shape, strip_parts[0][1].shape
    wide_size = strip_parts[0][0].size
    wide = jnp.concatenate(
        [side_lo[:wide_size].reshape(wide_shape), tall, side_hi[:wide_size].reshape(wide_shape)],
        axis=2,
    )
    ring = jnp.concatenate(
        [side_lo[wide_size:].reshape(k_shape), tall_k, side_hi[wide_size:].reshape(k_shape)],
        axis=1,
    )
    inner = ring[None] * laplace(wide)
    prior = laplace(inner)
    map_rows = directions.shape[1]
    map_cols = directions.shape[2]
    summed = jax.ops.segment_sum(
        got[:, :probes],
        got[:, probes].astype(jnp.int32),
        num_segments=map_rows * map_cols,
    )
    data = summed.T.reshape(probes, map_rows, map_cols)
    hessian = data + prior + 0.1 * directions
    return (image, hessian)


def solution(mesh):
    return jax.shard_map(
        shards,
        mesh=mesh,
        in_specs=(
            P(None, None, "layer", "mapx", "mapy"),
            P("layer", "mapx", "mapy"),
            P("mapx", "mapy"),
            P("mapx", "mapy", None, None),
            P("mapx", "mapy", None),
            P(None, "mapx", ("mapy", "layer")),
            P("mapx", ("mapy", "layer")),
        ),
        out_specs=(P(None, None, "layer", "mapx", "mapy"), P(None, "mapx", ("mapy", "layer"))),
        check_vma=False,
    )
```

```python
import jax
import jax.numpy as jnp
from jax import lax
from jax.sharding import PartitionSpec as P


def send(parts, axis, pairs):
    flat = jnp.concatenate([p.reshape(-1) for p in parts])
    got = lax.ppermute(flat, axis, pairs)
    out, at = [], 0
    for p in parts:
        out.append(got[at : at + p.size].reshape(p.shape))
        at += p.size
    return out


def steps(count):
    return [(i, i + 1) for i in range(count - 1)], [(i + 1, i) for i in range(count - 1)]


def pad_dims(part, dims):
    widths = [(0, 0)] * part.ndim
    for dim in dims:
        widths[dim] = (1, 1)
    return jnp.pad(part, widths)


def stencil(padded, viscous):
    center = padded[..., 1:-1, 1:-1, 1:-1]
    visc = viscous[1:-1, 1:-1, 1:-1]
    weight_x = jnp.array([1.0, 0.25], jnp.float32)[:, None, None, None]
    weight_y = jnp.array([0.25, 1.0], jnp.float32)[:, None, None, None]
    total = 2.0 * 0.5 * (visc + viscous[2:, 1:-1, 1:-1]) * (center - padded[..., 2:, 1:-1, 1:-1])
    total = total + 2.0 * 0.5 * (visc + viscous[:-2, 1:-1, 1:-1]) * (
        center - padded[..., :-2, 1:-1, 1:-1]
    )
    total = total + weight_x * 0.5 * (visc + viscous[1:-1, 2:, 1:-1]) * (
        center - padded[..., 1:-1, 2:, 1:-1]
    )
    total = total + weight_x * 0.5 * (visc + viscous[1:-1, :-2, 1:-1]) * (
        center - padded[..., 1:-1, :-2, 1:-1]
    )
    total = total + weight_y * 0.5 * (visc + viscous[1:-1, 1:-1, 2:]) * (
        center - padded[..., 1:-1, 1:-1, 2:]
    )
    total = total + weight_y * 0.5 * (visc + viscous[1:-1, 1:-1, :-2]) * (
        center - padded[..., 1:-1, 1:-1, :-2]
    )
    return total


def laplace(padded):
    return (
        4.0 * padded[..., 1:-1, 1:-1]
        - padded[..., 2:, 1:-1]
        - padded[..., :-2, 1:-1]
        - padded[..., 1:-1, 2:]
        - padded[..., 1:-1, :-2]
    )


def from_bottom(x, axis):
    count = lax.axis_size(axis)
    mine = lax.axis_index(axis) == 0
    total = jnp.where(mine, x, jnp.zeros_like(x))
    for to in range(1, count):
        total = total + lax.ppermute(x, axis, [(0, to)])
    return total


def slot_places(keys, group_count, capacity, keep):
    onehot = (
        (keys[:, None] == jnp.arange(group_count, dtype=jnp.int32)[None, :]) & keep[:, None]
    ).astype(jnp.int32)
    before = jnp.cumsum(onehot, axis=0) - onehot
    slot_index = jnp.sum(before * onehot, axis=1)
    return jnp.where(keep, keys * capacity + slot_index, group_count * capacity)


def shards(velocity, viscosity, friction, owner, cell, directions, stiffness):
    probes = velocity.shape[0]
    depth, rows, cols = viscosity.shape
    column = ("mapy", "layer")
    count_x = lax.axis_size("mapx")
    count_col = lax.axis_size(column)
    count_layer = lax.axis_size("layer")
    my_layer = lax.axis_index("layer")
    stacked = jnp.concatenate([velocity.reshape(probes * 2, depth, rows, cols), viscosity[None]], 0)
    fwd_x, bwd_x = steps(count_x)
    fwd_c, bwd_c = steps(count_col)
    fwd_y, bwd_y = steps(lax.axis_size("mapy"))
    d, k = directions, stiffness
    rmap = d.shape[1]
    fwd_l, bwd_l = steps(count_layer)
    x_lo = send([stacked[:, :, -1:], d[:, -2:], k[-1:]], "mapx", fwd_x)
    x_hi = send([stacked[:, :, :1], d[:, :2], k[:1]], "mapx", bwd_x)
    (z_lo,) = send([stacked[:, -1:]], "layer", fwd_l)
    (z_hi,) = send([stacked[:, :1]], "layer", bwd_l)
    (y_lo,) = send([stacked[..., -1:]], "mapy", fwd_y)
    (y_hi,) = send([stacked[..., :1]], "mapy", bwd_y)

    extended = jnp.concatenate([z_lo, stacked, z_hi], axis=1)
    extended = jnp.concatenate([pad_dims(x_lo[0], (1,)), extended, pad_dims(x_hi[0], (1,))], axis=2)
    extended = jnp.concatenate([pad_dims(y_lo, (1, 2)), extended, pad_dims(y_hi, (1, 2))], axis=3)
    padded = extended[:-1].reshape(probes, 2, depth + 2, rows + 2, cols + 2)
    image = stencil(padded, extended[-1])

    tall = jnp.concatenate([x_lo[1], d, x_hi[1]], axis=1)
    tall_k = jnp.concatenate([x_lo[2], k, x_hi[2]], axis=0)
    strip_parts = [
        (tall[:, 1 : rmap + 3, -1], tall[:, 2 : rmap + 2, -2], tall_k[1 : rmap + 1, -1]),
        (tall[:, 1 : rmap + 3, 0], tall[:, 2 : rmap + 2, 1], tall_k[1 : rmap + 1, 0]),
    ]

    face_count = rows * cols
    face_rows = (friction * (image[:, 0, 0] + image[:, 1, 0])).reshape(probes, face_count).T
    targets = owner.reshape(face_count)
    local_cells = cell.reshape(face_count).astype(jnp.float32)
    count_y = lax.axis_size("mapy")
    owner_count = count_y * count_layer
    capacity = 2 * face_count // owner_count
    onehot = (targets[:, None] == jnp.arange(owner_count, dtype=jnp.int32)[None, :]).astype(
        jnp.bfloat16
    )
    order = lax.broadcasted_iota(jnp.int32, (face_count, face_count), 0)
    earlier = (order > lax.broadcasted_iota(jnp.int32, (face_count, face_count), 1)).astype(
        jnp.bfloat16
    )
    before = jnp.dot(earlier, onehot, preferred_element_type=jnp.float32)
    rank = jnp.sum(before * onehot.astype(jnp.float32), axis=1).astype(jnp.int32)
    position = targets * capacity + rank
    total_slots = owner_count * capacity
    rows_out = jnp.concatenate([face_rows, local_cells[:, None]], axis=1)
    chooser = (
        lax.broadcasted_iota(jnp.int32, (total_slots, face_count), 0) == position[None, :]
    ).astype(jnp.float32)
    packed = jnp.dot(chooser, rows_out, precision=lax.Precision.HIGHEST)
    me = lax.axis_index(column)
    strips = [jnp.concatenate([p.reshape(-1) for p in parts]) for parts in strip_parts]
    strip_size = strips[0].size
    extra_rows = -(-strip_size // (probes + 1))
    strips = [
        jnp.pad(x, (0, extra_rows * (probes + 1) - strip_size)).reshape(extra_rows, probes + 1)
        for x in strips
    ]
    dest = lax.broadcasted_iota(jnp.int32, (owner_count, 1, 1), 0)
    extra = jnp.where(dest == me + 1, strips[0][None], 0.0) + jnp.where(
        dest == me - 1, strips[1][None], 0.0
    )
    packed = jnp.concatenate([packed.reshape(owner_count, capacity, probes + 1), extra], axis=1)
    received = lax.all_to_all(packed, column, split_axis=0, concat_axis=0, tiled=True)
    got = received[:, :capacity].reshape(count_y, count_layer, capacity, probes + 1)[:, 0]
    got = got.reshape(-1, probes + 1)
    side_lo = lax.dynamic_index_in_dim(received, jnp.maximum(me - 1, 0), 0, keepdims=False)
    side_hi = lax.dynamic_index_in_dim(
        received, jnp.minimum(me + 1, owner_count - 1), 0, keepdims=False
    )
    side_lo = jnp.where(me > 0, side_lo[capacity:], 0.0).reshape(-1)[:strip_size]
    side_hi = jnp.where(me < owner_count - 1, side_hi[capacity:], 0.0).reshape(-1)[:strip_size]
    sizes = [p.size for p in strip_parts[0]]

    def unpack(side):
        near = side[: sizes[0]].reshape(probes, rmap + 2)
        far = side[sizes[0] : sizes[0] + sizes[1]].reshape(probes, rmap)
        kk = side[sizes[0] + sizes[1] :]
        near = jnp.pad(near, ((0, 0), (1, 1)))[:, :, None]
        far = jnp.pad(far, ((0, 0), (2, 2)))[:, :, None]
        kk = jnp.pad(kk, (1, 1))[:, None]
        return near, far, kk

    lo_near, lo_far, lo_k = unpack(side_lo)
    hi_near, hi_far, hi_k = unpack(side_hi)
    wide = jnp.concatenate([lo_far, lo_near, tall, hi_near, hi_far], axis=2)
    ring = jnp.concatenate([lo_k, tall_k, hi_k], axis=1)
    inner = ring[None] * laplace(wide)
    prior = laplace(inner)
    map_rows = directions.shape[1]
    map_cols = directions.shape[2]
    places = got[:, probes].astype(jnp.int32)
    spots = (
        places[:, None] == lax.broadcasted_iota(jnp.int32, (1, map_rows * map_cols), 1)
    ).astype(jnp.float32)
    summed = jnp.dot(got[:, :probes].T, spots, precision=lax.Precision.HIGHEST)
    data = summed.reshape(probes, map_rows, map_cols)
    hessian = data + prior + 0.1 * directions
    return (image, hessian)


def solution(mesh):
    return jax.shard_map(
        shards,
        mesh=mesh,
        in_specs=(
            P(None, None, "layer", "mapx", "mapy"),
            P("layer", "mapx", "mapy"),
            P("mapx", "mapy"),
            P("mapx", "mapy", None, None),
            P("mapx", "mapy", None),
            P(None, "mapx", ("mapy", "layer")),
            P("mapx", ("mapy", "layer")),
        ),
        out_specs=(P(None, None, "layer", "mapx", "mapy"), P(None, "mapx", ("mapy", "layer"))),
        check_vma=False,
    )
```

```python
import jax
import jax.numpy as jnp
from jax import lax
from jax.sharding import PartitionSpec as P


def send(parts, axis, pairs):
    flat = jnp.concatenate([p.reshape(-1) for p in parts])
    got = lax.ppermute(flat, axis, pairs)
    out, at = [], 0
    for p in parts:
        out.append(got[at : at + p.size].reshape(p.shape))
        at += p.size
    return out


def steps(count):
    return [(i, i + 1) for i in range(count - 1)], [(i + 1, i) for i in range(count - 1)]


def pad_dims(part, dims):
    widths = [(0, 0)] * part.ndim
    for dim in dims:
        widths[dim] = (1, 1)
    return jnp.pad(part, widths)


def stencil(padded, viscous):
    center = padded[..., 1:-1, 1:-1, 1:-1]
    visc = viscous[1:-1, 1:-1, 1:-1]
    weight_x = jnp.array([1.0, 0.25], jnp.float32)[:, None, None, None]
    weight_y = jnp.array([0.25, 1.0], jnp.float32)[:, None, None, None]
    total = 2.0 * 0.5 * (visc + viscous[2:, 1:-1, 1:-1]) * (center - padded[..., 2:, 1:-1, 1:-1])
    total = total + 2.0 * 0.5 * (visc + viscous[:-2, 1:-1, 1:-1]) * (
        center - padded[..., :-2, 1:-1, 1:-1]
    )
    total = total + weight_x * 0.5 * (visc + viscous[1:-1, 2:, 1:-1]) * (
        center - padded[..., 1:-1, 2:, 1:-1]
    )
    total = total + weight_x * 0.5 * (visc + viscous[1:-1, :-2, 1:-1]) * (
        center - padded[..., 1:-1, :-2, 1:-1]
    )
    total = total + weight_y * 0.5 * (visc + viscous[1:-1, 1:-1, 2:]) * (
        center - padded[..., 1:-1, 1:-1, 2:]
    )
    total = total + weight_y * 0.5 * (visc + viscous[1:-1, 1:-1, :-2]) * (
        center - padded[..., 1:-1, 1:-1, :-2]
    )
    return total


def laplace(padded):
    return (
        4.0 * padded[..., 1:-1, 1:-1]
        - padded[..., 2:, 1:-1]
        - padded[..., :-2, 1:-1]
        - padded[..., 1:-1, 2:]
        - padded[..., 1:-1, :-2]
    )


def from_bottom(x, axis):
    count = lax.axis_size(axis)
    mine = lax.axis_index(axis) == 0
    total = jnp.where(mine, x, jnp.zeros_like(x))
    for to in range(1, count):
        total = total + lax.ppermute(x, axis, [(0, to)])
    return total


def slot_places(keys, group_count, capacity, keep):
    onehot = (
        (keys[:, None] == jnp.arange(group_count, dtype=jnp.int32)[None, :]) & keep[:, None]
    ).astype(jnp.int32)
    before = jnp.cumsum(onehot, axis=0) - onehot
    slot_index = jnp.sum(before * onehot, axis=1)
    return jnp.where(keep, keys * capacity + slot_index, group_count * capacity)


def shards(velocity, viscosity, friction, owner, cell, directions, stiffness):
    probes = velocity.shape[0]
    depth, rows, cols = viscosity.shape
    column = ("mapy", "layer")
    count_x = lax.axis_size("mapx")
    count_col = lax.axis_size(column)
    count_layer = lax.axis_size("layer")
    my_layer = lax.axis_index("layer")
    stacked = jnp.concatenate([velocity.reshape(probes * 2, depth, rows, cols), viscosity[None]], 0)
    face_count = rows * cols
    targets = owner.reshape(face_count)
    local_cells = cell.reshape(face_count).astype(jnp.float32)
    count_y = lax.axis_size("mapy")
    owner_count = count_y * count_layer
    capacity = 2 * face_count // owner_count
    onehot = (targets[:, None] == jnp.arange(owner_count, dtype=jnp.int32)[None, :]).astype(
        jnp.bfloat16
    )
    order = lax.broadcasted_iota(jnp.int32, (face_count, face_count), 0)
    earlier = (order > lax.broadcasted_iota(jnp.int32, (face_count, face_count), 1)).astype(
        jnp.bfloat16
    )
    before = jnp.dot(earlier, onehot, preferred_element_type=jnp.float32)
    rank = jnp.sum(before * onehot.astype(jnp.float32), axis=1).astype(jnp.int32)
    position = targets * capacity + rank
    total_slots = owner_count * capacity
    chooser = (
        lax.broadcasted_iota(jnp.int32, (total_slots, face_count), 0) == position[None, :]
    ).astype(jnp.bfloat16)
    fwd_x, bwd_x = steps(count_x)
    fwd_c, bwd_c = steps(count_col)
    fwd_y, bwd_y = steps(lax.axis_size("mapy"))
    d, k = directions, stiffness
    rmap = d.shape[1]
    fwd_l, bwd_l = steps(count_layer)
    x_lo = send([stacked[:, :, -1:], d[:, -2:], k[-1:]], "mapx", fwd_x)
    x_hi = send([stacked[:, :, :1], d[:, :2], k[:1]], "mapx", bwd_x)
    (z_lo,) = send([stacked[:, -1:]], "layer", fwd_l)
    (z_hi,) = send([stacked[:, :1]], "layer", bwd_l)
    (y_lo,) = send([stacked[..., -1:]], "mapy", fwd_y)
    (y_hi,) = send([stacked[..., :1]], "mapy", bwd_y)
    chooser, y_lo, y_hi = lax.optimization_barrier((chooser, y_lo, y_hi))

    extended = jnp.concatenate([z_lo, stacked, z_hi], axis=1)
    extended = jnp.concatenate([pad_dims(x_lo[0], (1,)), extended, pad_dims(x_hi[0], (1,))], axis=2)
    extended = jnp.concatenate([pad_dims(y_lo, (1, 2)), extended, pad_dims(y_hi, (1, 2))], axis=3)
    padded = extended[:-1].reshape(probes, 2, depth + 2, rows + 2, cols + 2)
    image = stencil(padded, extended[-1])

    tall = jnp.concatenate([x_lo[1], d, x_hi[1]], axis=1)
    tall_k = jnp.concatenate([x_lo[2], k, x_hi[2]], axis=0)
    strip_parts = [
        (tall[:, 1 : rmap + 3, -1], tall[:, 2 : rmap + 2, -2], tall_k[1 : rmap + 1, -1]),
        (tall[:, 1 : rmap + 3, 0], tall[:, 2 : rmap + 2, 1], tall_k[1 : rmap + 1, 0]),
    ]

    face_rows = (friction * (image[:, 0, 0] + image[:, 1, 0])).reshape(probes, face_count).T
    rows_out = jnp.concatenate([face_rows, local_cells[:, None]], axis=1)
    packed = jnp.dot(chooser.astype(jnp.float32), rows_out, precision=lax.Precision.HIGHEST)
    me = lax.axis_index(column)
    strips = [jnp.concatenate([p.reshape(-1) for p in parts]) for parts in strip_parts]
    strip_size = strips[0].size
    extra_rows = -(-strip_size // (probes + 1))
    strips = [
        jnp.pad(x, (0, extra_rows * (probes + 1) - strip_size)).reshape(extra_rows, probes + 1)
        for x in strips
    ]
    dest = lax.broadcasted_iota(jnp.int32, (owner_count, 1, 1), 0)
    extra = jnp.where(dest == me + 1, strips[0][None], 0.0) + jnp.where(
        dest == me - 1, strips[1][None], 0.0
    )
    packed = jnp.concatenate([packed.reshape(owner_count, capacity, probes + 1), extra], axis=1)
    received = lax.all_to_all(packed, column, split_axis=0, concat_axis=0, tiled=True)
    got = received[:, :capacity].reshape(count_y, count_layer, capacity, probes + 1)[:, 0]
    got = got.reshape(-1, probes + 1)
    side_lo = lax.dynamic_index_in_dim(received, jnp.maximum(me - 1, 0), 0, keepdims=False)
    side_hi = lax.dynamic_index_in_dim(
        received, jnp.minimum(me + 1, owner_count - 1), 0, keepdims=False
    )
    side_lo = jnp.where(me > 0, side_lo[capacity:], 0.0).reshape(-1)[:strip_size]
    side_hi = jnp.where(me < owner_count - 1, side_hi[capacity:], 0.0).reshape(-1)[:strip_size]
    sizes = [p.size for p in strip_parts[0]]

    def unpack(side):
        near = side[: sizes[0]].reshape(probes, rmap + 2)
        far = side[sizes[0] : sizes[0] + sizes[1]].reshape(probes, rmap)
        kk = side[sizes[0] + sizes[1] :]
        near = jnp.pad(near, ((0, 0), (1, 1)))[:, :, None]
        far = jnp.pad(far, ((0, 0), (2, 2)))[:, :, None]
        kk = jnp.pad(kk, (1, 1))[:, None]
        return near, far, kk

    lo_near, lo_far, lo_k = unpack(side_lo)
    hi_near, hi_far, hi_k = unpack(side_hi)
    wide = jnp.concatenate([lo_far, lo_near, tall, hi_near, hi_far], axis=2)
    ring = jnp.concatenate([lo_k, tall_k, hi_k], axis=1)
    inner = ring[None] * laplace(wide)
    prior = laplace(inner)
    map_rows = directions.shape[1]
    map_cols = directions.shape[2]
    places = got[:, probes].astype(jnp.int32)
    spots = (
        places[:, None] == lax.broadcasted_iota(jnp.int32, (1, map_rows * map_cols), 1)
    ).astype(jnp.float32)
    summed = jnp.dot(got[:, :probes].T, spots, precision=lax.Precision.HIGHEST)
    data = summed.reshape(probes, map_rows, map_cols)
    hessian = data + prior + 0.1 * directions
    return (image, hessian)


def solution(mesh):
    return jax.shard_map(
        shards,
        mesh=mesh,
        in_specs=(
            P(None, None, "layer", "mapx", "mapy"),
            P("layer", "mapx", "mapy"),
            P("mapx", "mapy"),
            P("mapx", "mapy", None, None),
            P("mapx", "mapy", None),
            P(None, "mapx", ("mapy", "layer")),
            P("mapx", ("mapy", "layer")),
        ),
        out_specs=(P(None, None, "layer", "mapx", "mapy"), P(None, "mapx", ("mapy", "layer"))),
        check_vma=False,
    )
```

```python
import jax
import jax.numpy as jnp
from jax import lax
from jax.sharding import PartitionSpec as P


def send(parts, axis, pairs):
    flat = jnp.concatenate([p.reshape(-1) for p in parts])
    got = lax.ppermute(flat, axis, pairs)
    out, at = [], 0
    for p in parts:
        out.append(got[at : at + p.size].reshape(p.shape))
        at += p.size
    return out


def steps(count):
    return [(i, i + 1) for i in range(count - 1)], [(i + 1, i) for i in range(count - 1)]


def pad_dims(part, dims):
    widths = [(0, 0)] * part.ndim
    for dim in dims:
        widths[dim] = (1, 1)
    return jnp.pad(part, widths)


def stencil(padded, viscous):
    center = padded[..., 1:-1, 1:-1, 1:-1]
    visc = viscous[1:-1, 1:-1, 1:-1]
    weight_x = jnp.array([1.0, 0.25], jnp.float32)[:, None, None, None]
    weight_y = jnp.array([0.25, 1.0], jnp.float32)[:, None, None, None]
    total = 2.0 * 0.5 * (visc + viscous[2:, 1:-1, 1:-1]) * (center - padded[..., 2:, 1:-1, 1:-1])
    total = total + 2.0 * 0.5 * (visc + viscous[:-2, 1:-1, 1:-1]) * (
        center - padded[..., :-2, 1:-1, 1:-1]
    )
    total = total + weight_x * 0.5 * (visc + viscous[1:-1, 2:, 1:-1]) * (
        center - padded[..., 1:-1, 2:, 1:-1]
    )
    total = total + weight_x * 0.5 * (visc + viscous[1:-1, :-2, 1:-1]) * (
        center - padded[..., 1:-1, :-2, 1:-1]
    )
    total = total + weight_y * 0.5 * (visc + viscous[1:-1, 1:-1, 2:]) * (
        center - padded[..., 1:-1, 1:-1, 2:]
    )
    total = total + weight_y * 0.5 * (visc + viscous[1:-1, 1:-1, :-2]) * (
        center - padded[..., 1:-1, 1:-1, :-2]
    )
    return total


def laplace(padded):
    return (
        4.0 * padded[..., 1:-1, 1:-1]
        - padded[..., 2:, 1:-1]
        - padded[..., :-2, 1:-1]
        - padded[..., 1:-1, 2:]
        - padded[..., 1:-1, :-2]
    )


def from_bottom(x, axis):
    count = lax.axis_size(axis)
    mine = lax.axis_index(axis) == 0
    total = jnp.where(mine, x, jnp.zeros_like(x))
    for to in range(1, count):
        total = total + lax.ppermute(x, axis, [(0, to)])
    return total


def slot_places(keys, group_count, capacity, keep):
    onehot = (
        (keys[:, None] == jnp.arange(group_count, dtype=jnp.int32)[None, :]) & keep[:, None]
    ).astype(jnp.int32)
    before = jnp.cumsum(onehot, axis=0) - onehot
    slot_index = jnp.sum(before * onehot, axis=1)
    return jnp.where(keep, keys * capacity + slot_index, group_count * capacity)


def shards(velocity, viscosity, friction, owner, cell, directions, stiffness):
    probes = velocity.shape[0]
    depth, rows, cols = viscosity.shape
    column = ("mapy", "layer")
    count_x = lax.axis_size("mapx")
    count_col = lax.axis_size(column)
    count_layer = lax.axis_size("layer")
    my_layer = lax.axis_index("layer")
    stacked = jnp.concatenate([velocity.reshape(probes * 2, depth, rows, cols), viscosity[None]], 0)
    fwd_x, bwd_x = steps(count_x)
    fwd_c, bwd_c = steps(count_col)
    fwd_y, bwd_y = steps(lax.axis_size("mapy"))
    d, k = directions, stiffness
    rmap = d.shape[1]
    fwd_l, bwd_l = steps(count_layer)
    x_lo = send([stacked[:, :, -1:], d[:, -2:], k[-1:]], "mapx", fwd_x)
    x_hi = send([stacked[:, :, :1], d[:, :2], k[:1]], "mapx", bwd_x)
    (z_lo,) = send([stacked[:, -1:]], "layer", fwd_l)
    (z_hi,) = send([stacked[:, :1]], "layer", bwd_l)
    (y_lo,) = send([stacked[..., -1:]], "mapy", fwd_y)
    (y_hi,) = send([stacked[..., :1]], "mapy", bwd_y)

    extended = jnp.concatenate([z_lo, stacked, z_hi], axis=1)
    extended = jnp.concatenate([pad_dims(x_lo[0], (1,)), extended, pad_dims(x_hi[0], (1,))], axis=2)
    extended = jnp.concatenate([pad_dims(y_lo, (1, 2)), extended, pad_dims(y_hi, (1, 2))], axis=3)
    padded = extended[:-1].reshape(probes, 2, depth + 2, rows + 2, cols + 2)
    image = stencil(padded, extended[-1])

    tall = jnp.concatenate([x_lo[1], d, x_hi[1]], axis=1)
    tall_k = jnp.concatenate([x_lo[2], k, x_hi[2]], axis=0)
    strip_parts = [
        (tall[:, 1 : rmap + 3, -1], tall[:, 2 : rmap + 2, -2], tall_k[1 : rmap + 1, -1]),
        (tall[:, 1 : rmap + 3, 0], tall[:, 2 : rmap + 2, 1], tall_k[1 : rmap + 1, 0]),
    ]

    face_count = rows * cols
    face_rows = (friction * (image[:, 0, 0] + image[:, 1, 0])).reshape(probes, face_count).T
    targets = owner.reshape(face_count)
    local_cells = cell.reshape(face_count).astype(jnp.float32)
    count_y = lax.axis_size("mapy")
    owner_count = count_y * count_layer
    capacity = 2 * face_count // owner_count
    onehot = (targets[:, None] == jnp.arange(owner_count, dtype=jnp.int32)[None, :]).astype(
        jnp.bfloat16
    )
    order = lax.broadcasted_iota(jnp.int32, (face_count, face_count), 0)
    earlier = (order > lax.broadcasted_iota(jnp.int32, (face_count, face_count), 1)).astype(
        jnp.bfloat16
    )
    before = jnp.dot(earlier, onehot, preferred_element_type=jnp.float32)
    rank = jnp.sum(before * onehot.astype(jnp.float32), axis=1).astype(jnp.int32)
    position = targets * capacity + rank
    total_slots = owner_count * capacity
    rows_out = jnp.concatenate([face_rows, local_cells[:, None]], axis=1)
    source = jnp.full((total_slots,), face_count, jnp.int32).at[position].set(
        jnp.arange(face_count, dtype=jnp.int32), mode="drop"
    )
    rows_out = jnp.concatenate([rows_out, jnp.zeros((1, probes + 1), jnp.float32)], axis=0)
    packed = jnp.take(rows_out, source, axis=0, mode="clip")
    me = lax.axis_index(column)
    strips = [jnp.concatenate([p.reshape(-1) for p in parts]) for parts in strip_parts]
    strip_size = strips[0].size
    extra_rows = -(-strip_size // (probes + 1))
    strips = [
        jnp.pad(x, (0, extra_rows * (probes + 1) - strip_size)).reshape(extra_rows, probes + 1)
        for x in strips
    ]
    dest = lax.broadcasted_iota(jnp.int32, (owner_count, 1, 1), 0)
    extra = jnp.where(dest == me + 1, strips[0][None], 0.0) + jnp.where(
        dest == me - 1, strips[1][None], 0.0
    )
    packed = jnp.concatenate([packed.reshape(owner_count, capacity, probes + 1), extra], axis=1)
    received = lax.all_to_all(packed, column, split_axis=0, concat_axis=0, tiled=True)
    got = received[:, :capacity].reshape(count_y, count_layer, capacity, probes + 1)[:, 0]
    got = got.reshape(-1, probes + 1)
    side_lo = lax.dynamic_index_in_dim(received, jnp.maximum(me - 1, 0), 0, keepdims=False)
    side_hi = lax.dynamic_index_in_dim(
        received, jnp.minimum(me + 1, owner_count - 1), 0, keepdims=False
    )
    side_lo = jnp.where(me > 0, side_lo[capacity:], 0.0).reshape(-1)[:strip_size]
    side_hi = jnp.where(me < owner_count - 1, side_hi[capacity:], 0.0).reshape(-1)[:strip_size]
    sizes = [p.size for p in strip_parts[0]]

    def unpack(side):
        near = side[: sizes[0]].reshape(probes, rmap + 2)
        far = side[sizes[0] : sizes[0] + sizes[1]].reshape(probes, rmap)
        kk = side[sizes[0] + sizes[1] :]
        near = jnp.pad(near, ((0, 0), (1, 1)))[:, :, None]
        far = jnp.pad(far, ((0, 0), (2, 2)))[:, :, None]
        kk = jnp.pad(kk, (1, 1))[:, None]
        return near, far, kk

    lo_near, lo_far, lo_k = unpack(side_lo)
    hi_near, hi_far, hi_k = unpack(side_hi)
    wide = jnp.concatenate([lo_far, lo_near, tall, hi_near, hi_far], axis=2)
    ring = jnp.concatenate([lo_k, tall_k, hi_k], axis=1)
    inner = ring[None] * laplace(wide)
    prior = laplace(inner)
    map_rows = directions.shape[1]
    map_cols = directions.shape[2]
    places = got[:, probes].astype(jnp.int32)
    spots = (
        places[:, None] == lax.broadcasted_iota(jnp.int32, (1, map_rows * map_cols), 1)
    ).astype(jnp.float32)
    summed = jnp.dot(got[:, :probes].T, spots, precision=lax.Precision.HIGHEST)
    data = summed.reshape(probes, map_rows, map_cols)
    hessian = data + prior + 0.1 * directions
    return (image, hessian)


def solution(mesh):
    return jax.shard_map(
        shards,
        mesh=mesh,
        in_specs=(
            P(None, None, "layer", "mapx", "mapy"),
            P("layer", "mapx", "mapy"),
            P("mapx", "mapy"),
            P("mapx", "mapy", None, None),
            P("mapx", "mapy", None),
            P(None, "mapx", ("mapy", "layer")),
            P("mapx", ("mapy", "layer")),
        ),
        out_specs=(P(None, None, "layer", "mapx", "mapy"), P(None, "mapx", ("mapy", "layer"))),
        check_vma=False,
    )
```

```python
import jax
import jax.numpy as jnp
from jax import lax
from jax.sharding import PartitionSpec as P


def send(parts, axis, pairs):
    flat = jnp.concatenate([p.reshape(-1) for p in parts])
    got = lax.ppermute(flat, axis, pairs)
    out, at = [], 0
    for p in parts:
        out.append(got[at : at + p.size].reshape(p.shape))
        at += p.size
    return out


def steps(count):
    return [(i, i + 1) for i in range(count - 1)], [(i + 1, i) for i in range(count - 1)]


def pad_dims(part, dims):
    widths = [(0, 0)] * part.ndim
    for dim in dims:
        widths[dim] = (1, 1)
    return jnp.pad(part, widths)


def stencil(padded, viscous):
    center = padded[..., 1:-1, 1:-1, 1:-1]
    visc = viscous[1:-1, 1:-1, 1:-1]
    weight_x = jnp.array([1.0, 0.25], jnp.float32)[:, None, None, None]
    weight_y = jnp.array([0.25, 1.0], jnp.float32)[:, None, None, None]
    total = 2.0 * 0.5 * (visc + viscous[2:, 1:-1, 1:-1]) * (center - padded[..., 2:, 1:-1, 1:-1])
    total = total + 2.0 * 0.5 * (visc + viscous[:-2, 1:-1, 1:-1]) * (
        center - padded[..., :-2, 1:-1, 1:-1]
    )
    total = total + weight_x * 0.5 * (visc + viscous[1:-1, 2:, 1:-1]) * (
        center - padded[..., 1:-1, 2:, 1:-1]
    )
    total = total + weight_x * 0.5 * (visc + viscous[1:-1, :-2, 1:-1]) * (
        center - padded[..., 1:-1, :-2, 1:-1]
    )
    total = total + weight_y * 0.5 * (visc + viscous[1:-1, 1:-1, 2:]) * (
        center - padded[..., 1:-1, 1:-1, 2:]
    )
    total = total + weight_y * 0.5 * (visc + viscous[1:-1, 1:-1, :-2]) * (
        center - padded[..., 1:-1, 1:-1, :-2]
    )
    return total


def laplace(padded):
    return (
        4.0 * padded[..., 1:-1, 1:-1]
        - padded[..., 2:, 1:-1]
        - padded[..., :-2, 1:-1]
        - padded[..., 1:-1, 2:]
        - padded[..., 1:-1, :-2]
    )


def from_bottom(x, axis):
    count = lax.axis_size(axis)
    mine = lax.axis_index(axis) == 0
    total = jnp.where(mine, x, jnp.zeros_like(x))
    for to in range(1, count):
        total = total + lax.ppermute(x, axis, [(0, to)])
    return total


def slot_places(keys, group_count, capacity, keep):
    onehot = (
        (keys[:, None] == jnp.arange(group_count, dtype=jnp.int32)[None, :]) & keep[:, None]
    ).astype(jnp.int32)
    before = jnp.cumsum(onehot, axis=0) - onehot
    slot_index = jnp.sum(before * onehot, axis=1)
    return jnp.where(keep, keys * capacity + slot_index, group_count * capacity)


def shards(velocity, viscosity, friction, owner, cell, directions, stiffness):
    probes = velocity.shape[0]
    depth, rows, cols = viscosity.shape
    column = ("mapy", "layer")
    count_x = lax.axis_size("mapx")
    count_col = lax.axis_size(column)
    count_layer = lax.axis_size("layer")
    my_layer = lax.axis_index("layer")
    stacked = jnp.concatenate([velocity.reshape(probes * 2, depth, rows, cols), viscosity[None]], 0)
    fwd_x, bwd_x = steps(count_x)
    fwd_c, bwd_c = steps(count_col)
    fwd_y, bwd_y = steps(lax.axis_size("mapy"))
    d, k = directions, stiffness
    rmap = d.shape[1]
    fwd_l, bwd_l = steps(count_layer)
    x_lo = send([stacked[:, :, -1:], d[:, -2:], k[-1:]], "mapx", fwd_x)
    x_hi = send([stacked[:, :, :1], d[:, :2], k[:1]], "mapx", bwd_x)
    (z_lo,) = send([stacked[:, -1:]], "layer", fwd_l)
    (z_hi,) = send([stacked[:, :1]], "layer", bwd_l)
    (y_lo,) = send([stacked[..., -1:]], "mapy", fwd_y)
    (y_hi,) = send([stacked[..., :1]], "mapy", bwd_y)

    extended = jnp.concatenate([z_lo, stacked, z_hi], axis=1)
    extended = jnp.concatenate([pad_dims(x_lo[0], (1,)), extended, pad_dims(x_hi[0], (1,))], axis=2)
    extended = jnp.concatenate([pad_dims(y_lo, (1, 2)), extended, pad_dims(y_hi, (1, 2))], axis=3)
    padded = extended[:-1].reshape(probes, 2, depth + 2, rows + 2, cols + 2)
    image = stencil(padded, extended[-1])

    tall = jnp.concatenate([x_lo[1], d, x_hi[1]], axis=1)
    tall_k = jnp.concatenate([x_lo[2], k, x_hi[2]], axis=0)
    strip_parts = [
        (tall[:, 1 : rmap + 3, -1], tall[:, 2 : rmap + 2, -2], tall_k[1 : rmap + 1, -1]),
        (tall[:, 1 : rmap + 3, 0], tall[:, 2 : rmap + 2, 1], tall_k[1 : rmap + 1, 0]),
    ]

    face_count = rows * cols
    face_rows = (friction * (image[:, 0, 0] + image[:, 1, 0])).reshape(probes, face_count).T
    targets = owner.reshape(face_count)
    local_cells = cell.reshape(face_count).astype(jnp.float32)
    count_y = lax.axis_size("mapy")
    owner_count = count_y * count_layer
    capacity = 2 * face_count // owner_count
    onehot = (targets[:, None] == jnp.arange(owner_count, dtype=jnp.int32)[None, :]).astype(
        jnp.bfloat16
    )
    order = lax.broadcasted_iota(jnp.int32, (face_count, face_count), 0)
    earlier = (order > lax.broadcasted_iota(jnp.int32, (face_count, face_count), 1)).astype(
        jnp.bfloat16
    )
    before = jnp.dot(earlier, onehot, preferred_element_type=jnp.float32)
    rank = jnp.sum(before * onehot.astype(jnp.float32), axis=1).astype(jnp.int32)
    position = targets * capacity + rank
    total_slots = owner_count * capacity
    rows_out = jnp.concatenate([face_rows, local_cells[:, None]], axis=1)
    chooser = (
        lax.broadcasted_iota(jnp.int32, (total_slots, face_count), 0) == position[None, :]
    ).astype(jnp.float32)
    packed = jnp.dot(chooser, rows_out, precision=lax.Precision.HIGH)
    me = lax.axis_index(column)
    strips = [jnp.concatenate([p.reshape(-1) for p in parts]) for parts in strip_parts]
    strip_size = strips[0].size
    extra_rows = -(-strip_size // (probes + 1))
    strips = [
        jnp.pad(x, (0, extra_rows * (probes + 1) - strip_size)).reshape(extra_rows, probes + 1)
        for x in strips
    ]
    dest = lax.broadcasted_iota(jnp.int32, (owner_count, 1, 1), 0)
    extra = jnp.where(dest == me + 1, strips[0][None], 0.0) + jnp.where(
        dest == me - 1, strips[1][None], 0.0
    )
    packed = jnp.concatenate([packed.reshape(owner_count, capacity, probes + 1), extra], axis=1)
    received = lax.all_to_all(packed, column, split_axis=0, concat_axis=0, tiled=True)
    got = received[:, :capacity].reshape(count_y, count_layer, capacity, probes + 1)[:, 0]
    got = got.reshape(-1, probes + 1)
    side_lo = lax.dynamic_index_in_dim(received, jnp.maximum(me - 1, 0), 0, keepdims=False)
    side_hi = lax.dynamic_index_in_dim(
        received, jnp.minimum(me + 1, owner_count - 1), 0, keepdims=False
    )
    side_lo = jnp.where(me > 0, side_lo[capacity:], 0.0).reshape(-1)[:strip_size]
    side_hi = jnp.where(me < owner_count - 1, side_hi[capacity:], 0.0).reshape(-1)[:strip_size]
    sizes = [p.size for p in strip_parts[0]]

    def unpack(side):
        near = side[: sizes[0]].reshape(probes, rmap + 2)
        far = side[sizes[0] : sizes[0] + sizes[1]].reshape(probes, rmap)
        kk = side[sizes[0] + sizes[1] :]
        near = jnp.pad(near, ((0, 0), (1, 1)))[:, :, None]
        far = jnp.pad(far, ((0, 0), (2, 2)))[:, :, None]
        kk = jnp.pad(kk, (1, 1))[:, None]
        return near, far, kk

    lo_near, lo_far, lo_k = unpack(side_lo)
    hi_near, hi_far, hi_k = unpack(side_hi)
    wide = jnp.concatenate([lo_far, lo_near, tall, hi_near, hi_far], axis=2)
    ring = jnp.concatenate([lo_k, tall_k, hi_k], axis=1)
    inner = ring[None] * laplace(wide)
    prior = laplace(inner)
    map_rows = directions.shape[1]
    map_cols = directions.shape[2]
    places = jnp.round(got[:, probes]).astype(jnp.int32)
    spots = (
        places[:, None] == lax.broadcasted_iota(jnp.int32, (1, map_rows * map_cols), 1)
    ).astype(jnp.float32)
    summed = jnp.dot(got[:, :probes].T, spots, precision=lax.Precision.HIGHEST)
    data = summed.reshape(probes, map_rows, map_cols)
    hessian = data + prior + 0.1 * directions
    return (image, hessian)


def solution(mesh):
    return jax.shard_map(
        shards,
        mesh=mesh,
        in_specs=(
            P(None, None, "layer", "mapx", "mapy"),
            P("layer", "mapx", "mapy"),
            P("mapx", "mapy"),
            P("mapx", "mapy", None, None),
            P("mapx", "mapy", None),
            P(None, "mapx", ("mapy", "layer")),
            P("mapx", ("mapy", "layer")),
        ),
        out_specs=(P(None, None, "layer", "mapx", "mapy"), P(None, "mapx", ("mapy", "layer"))),
        check_vma=False,
    )
```

```python
import jax
import jax.numpy as jnp
from jax import lax
from jax.sharding import PartitionSpec as P


def send(parts, axis, pairs):
    flat = jnp.concatenate([p.reshape(-1) for p in parts])
    got = lax.ppermute(flat, axis, pairs)
    out, at = [], 0
    for p in parts:
        out.append(got[at : at + p.size].reshape(p.shape))
        at += p.size
    return out


def steps(count):
    return [(i, i + 1) for i in range(count - 1)], [(i + 1, i) for i in range(count - 1)]


def pad_dims(part, dims):
    widths = [(0, 0)] * part.ndim
    for dim in dims:
        widths[dim] = (1, 1)
    return jnp.pad(part, widths)


def stencil(padded, viscous):
    center = padded[..., 1:-1, 1:-1, 1:-1]
    visc = viscous[1:-1, 1:-1, 1:-1]
    weight_x = jnp.array([1.0, 0.25], jnp.float32)[:, None, None, None]
    weight_y = jnp.array([0.25, 1.0], jnp.float32)[:, None, None, None]
    total = 2.0 * 0.5 * (visc + viscous[2:, 1:-1, 1:-1]) * (center - padded[..., 2:, 1:-1, 1:-1])
    total = total + 2.0 * 0.5 * (visc + viscous[:-2, 1:-1, 1:-1]) * (
        center - padded[..., :-2, 1:-1, 1:-1]
    )
    total = total + weight_x * 0.5 * (visc + viscous[1:-1, 2:, 1:-1]) * (
        center - padded[..., 1:-1, 2:, 1:-1]
    )
    total = total + weight_x * 0.5 * (visc + viscous[1:-1, :-2, 1:-1]) * (
        center - padded[..., 1:-1, :-2, 1:-1]
    )
    total = total + weight_y * 0.5 * (visc + viscous[1:-1, 1:-1, 2:]) * (
        center - padded[..., 1:-1, 1:-1, 2:]
    )
    total = total + weight_y * 0.5 * (visc + viscous[1:-1, 1:-1, :-2]) * (
        center - padded[..., 1:-1, 1:-1, :-2]
    )
    return total


def laplace(padded):
    return (
        4.0 * padded[..., 1:-1, 1:-1]
        - padded[..., 2:, 1:-1]
        - padded[..., :-2, 1:-1]
        - padded[..., 1:-1, 2:]
        - padded[..., 1:-1, :-2]
    )


def from_bottom(x, axis):
    count = lax.axis_size(axis)
    mine = lax.axis_index(axis) == 0
    total = jnp.where(mine, x, jnp.zeros_like(x))
    for to in range(1, count):
        total = total + lax.ppermute(x, axis, [(0, to)])
    return total


def slot_places(keys, group_count, capacity, keep):
    onehot = (
        (keys[:, None] == jnp.arange(group_count, dtype=jnp.int32)[None, :]) & keep[:, None]
    ).astype(jnp.int32)
    before = jnp.cumsum(onehot, axis=0) - onehot
    slot_index = jnp.sum(before * onehot, axis=1)
    return jnp.where(keep, keys * capacity + slot_index, group_count * capacity)


def shards(velocity, viscosity, friction, owner, cell, directions, stiffness):
    probes = velocity.shape[0]
    depth, rows, cols = viscosity.shape
    column = ("mapy", "layer")
    count_x = lax.axis_size("mapx")
    count_col = lax.axis_size(column)
    count_layer = lax.axis_size("layer")
    my_layer = lax.axis_index("layer")
    stacked = jnp.concatenate([velocity.reshape(probes * 2, depth, rows, cols), viscosity[None]], 0)
    fwd_x, bwd_x = steps(count_x)
    fwd_c, bwd_c = steps(count_col)
    fwd_y, bwd_y = steps(lax.axis_size("mapy"))
    d, k = directions, stiffness
    rmap = d.shape[1]
    fwd_l, bwd_l = steps(count_layer)
    x_lo = send([stacked[:, :, -1:], d[:, -2:], k[-1:]], "mapx", fwd_x)
    x_hi = send([stacked[:, :, :1], d[:, :2], k[:1]], "mapx", bwd_x)
    (z_lo,) = send([stacked[:, -1:]], "layer", fwd_l)
    (z_hi,) = send([stacked[:, :1]], "layer", bwd_l)
    (y_lo,) = send([stacked[..., -1:]], "mapy", fwd_y)
    (y_hi,) = send([stacked[..., :1]], "mapy", bwd_y)

    extended = jnp.concatenate([z_lo, stacked, z_hi], axis=1)
    extended = jnp.concatenate([pad_dims(x_lo[0], (1,)), extended, pad_dims(x_hi[0], (1,))], axis=2)
    extended = jnp.concatenate([pad_dims(y_lo, (1, 2)), extended, pad_dims(y_hi, (1, 2))], axis=3)
    padded = extended[:-1].reshape(probes, 2, depth + 2, rows + 2, cols + 2)
    image = stencil(padded, extended[-1])

    tall = jnp.concatenate([x_lo[1], d, x_hi[1]], axis=1)
    tall_k = jnp.concatenate([x_lo[2], k, x_hi[2]], axis=0)
    strip_parts = [
        (tall[:, 1 : rmap + 3, -1], tall[:, 2 : rmap + 2, -2], tall_k[1 : rmap + 1, -1]),
        (tall[:, 1 : rmap + 3, 0], tall[:, 2 : rmap + 2, 1], tall_k[1 : rmap + 1, 0]),
    ]

    face_count = rows * cols
    face_rows = (friction * (image[:, 0, 0] + image[:, 1, 0])).reshape(probes, face_count).T
    targets = owner.reshape(face_count)
    local_cells = cell.reshape(face_count).astype(jnp.float32)
    count_y = lax.axis_size("mapy")
    owner_count = count_y * count_layer
    capacity = 2 * face_count // owner_count
    onehot = (targets[:, None] == jnp.arange(owner_count, dtype=jnp.int32)[None, :]).astype(
        jnp.bfloat16
    )
    order = lax.broadcasted_iota(jnp.int32, (face_count, face_count), 0)
    earlier = (order > lax.broadcasted_iota(jnp.int32, (face_count, face_count), 1)).astype(
        jnp.bfloat16
    )
    before = jnp.dot(earlier, onehot, preferred_element_type=jnp.float32)
    rank = jnp.sum(before * onehot.astype(jnp.float32), axis=1).astype(jnp.int32)
    position = targets * capacity + rank
    total_slots = owner_count * capacity
    rows_out = jnp.concatenate([face_rows, local_cells[:, None]], axis=1)
    chooser = (
        position[:, None] == lax.broadcasted_iota(jnp.int32, (face_count, total_slots), 1)
    ).astype(jnp.float32)
    packed = jnp.dot(rows_out.T, chooser, precision=lax.Precision.HIGHEST).T
    me = lax.axis_index(column)
    strips = [jnp.concatenate([p.reshape(-1) for p in parts]) for parts in strip_parts]
    strip_size = strips[0].size
    extra_rows = -(-strip_size // (probes + 1))
    strips = [
        jnp.pad(x, (0, extra_rows * (probes + 1) - strip_size)).reshape(extra_rows, probes + 1)
        for x in strips
    ]
    dest = lax.broadcasted_iota(jnp.int32, (owner_count, 1, 1), 0)
    extra = jnp.where(dest == me + 1, strips[0][None], 0.0) + jnp.where(
        dest == me - 1, strips[1][None], 0.0
    )
    packed = jnp.concatenate([packed.reshape(owner_count, capacity, probes + 1), extra], axis=1)
    received = lax.all_to_all(packed, column, split_axis=0, concat_axis=0, tiled=True)
    got = received[:, :capacity].reshape(count_y, count_layer, capacity, probes + 1)[:, 0]
    got = got.reshape(-1, probes + 1)
    side_lo = lax.dynamic_index_in_dim(received, jnp.maximum(me - 1, 0), 0, keepdims=False)
    side_hi = lax.dynamic_index_in_dim(
        received, jnp.minimum(me + 1, owner_count - 1), 0, keepdims=False
    )
    side_lo = jnp.where(me > 0, side_lo[capacity:], 0.0).reshape(-1)[:strip_size]
    side_hi = jnp.where(me < owner_count - 1, side_hi[capacity:], 0.0).reshape(-1)[:strip_size]
    sizes = [p.size for p in strip_parts[0]]

    def unpack(side):
        near = side[: sizes[0]].reshape(probes, rmap + 2)
        far = side[sizes[0] : sizes[0] + sizes[1]].reshape(probes, rmap)
        kk = side[sizes[0] + sizes[1] :]
        near = jnp.pad(near, ((0, 0), (1, 1)))[:, :, None]
        far = jnp.pad(far, ((0, 0), (2, 2)))[:, :, None]
        kk = jnp.pad(kk, (1, 1))[:, None]
        return near, far, kk

    lo_near, lo_far, lo_k = unpack(side_lo)
    hi_near, hi_far, hi_k = unpack(side_hi)
    wide = jnp.concatenate([lo_far, lo_near, tall, hi_near, hi_far], axis=2)
    ring = jnp.concatenate([lo_k, tall_k, hi_k], axis=1)
    inner = ring[None] * laplace(wide)
    prior = laplace(inner)
    map_rows = directions.shape[1]
    map_cols = directions.shape[2]
    places = got[:, probes].astype(jnp.int32)
    spots = (
        places[:, None] == lax.broadcasted_iota(jnp.int32, (1, map_rows * map_cols), 1)
    ).astype(jnp.float32)
    summed = jnp.dot(got[:, :probes].T, spots, precision=lax.Precision.HIGHEST)
    data = summed.reshape(probes, map_rows, map_cols)
    hessian = data + prior + 0.1 * directions
    return (image, hessian)


def solution(mesh):
    return jax.shard_map(
        shards,
        mesh=mesh,
        in_specs=(
            P(None, None, "layer", "mapx", "mapy"),
            P("layer", "mapx", "mapy"),
            P("mapx", "mapy"),
            P("mapx", "mapy", None, None),
            P("mapx", "mapy", None),
            P(None, "mapx", ("mapy", "layer")),
            P("mapx", ("mapy", "layer")),
        ),
        out_specs=(P(None, None, "layer", "mapx", "mapy"), P(None, "mapx", ("mapy", "layer"))),
        check_vma=False,
    )
```
